256 devices in a mesh: dp: 8 (over x, core), ev: 32 (over y, z).
Axes of the slice: x: 4, y: 4, z: 8, core: 2. Of those that a mesh axis runs over, the one named last changes fastest.
Arguments:
- events: bfloat16 [8, 4096, 512], P('dp', 'ev'), may hold values from -25 to 25
- cotangent: bfloat16 [8, 4096, 512], P('dp', 'ev'), may hold values from -6 to 6
- intra_gain: float32 [512], replicated, may hold values from 0.25 to 1.75
- intra_proj: bfloat16 [512, 1536], replicated, may hold values from -27 to 27
- intra_out: bfloat16 [512, 512], replicated, may hold values from -0.25 to 0.25
- cross_norm_gain: float32 [512], replicated, may hold values from 0.25 to 1.75
- cross_input_weight: bfloat16 [512, 1536], replicated, may hold values from -27 to 27
- cross_output_weight: bfloat16 [512, 512], replicated, may hold values from -0.25 to 0.25
- owner_map: int32 [8, 4096], P('dp'), may hold values from 0 to 31, as said below
- block_lists: int32 [8, 32, 2, 2], P('dp', 'ev'), may hold values from 0 to 1
Outputs:
- layer_out: bfloat16 [8, 4096, 512], P('dp', 'ev')
- grad_events: bfloat16 [8, 4096, 512], P('dp', 'ev')
- grad_cross_proj: float32 [512, 1536], P('ev')
- grad_cross_out: float32 [512, 512], P('ev')
The draws below stay inside these ranges and needn't reach their ends.
Inputs may be any that keep to these rules, and one draw needn't show every extreme that they name: `owner_map`: in each replica no device sends more than 8 rows to one owner.
All inputs are finite; a program needn't handle non-finite values.
Results may differ from the reference program's by a relative error of at most 0.033.
The reference program's roundings to bfloat16 on the way count: a program that leaves them out, or rounds other values in their place, can miss the bound.
Values may be sent and summed in bfloat16 or wider, within the bound.
No kernel may reach another device: no remote copies, remote signals or barrier semaphores. Data moves between devices by JAX's collectives and lax.ppermute only.
A program may use at most 64 MiB of HBM per device.

```python
import math
import jax
import jax.numpy as jnp
from jax import lax

D = 512
HEADS = 8
HEAD_DIM = 64
EVENTS_PER_BLOCK = 128
KB = 2
ROWS_DEV = 128
REPLICAS = 8
OWNER_DEVICES = 32
ROWS = 4096
SEND_LIMIT = 8
RECEIVE_ROWS = 256
NRB = 2


def draw_events(key, part):
    base_key = jax.random.fold_in(key, 101)
    subkeys = jax.random.split(base_key, 3)
    row_scale = jnp.exp(jax.random.uniform(subkeys[0], (REPLICAS, ROWS, 1), jnp.float32, math.log(0.5), math.log(2.5)))
    col_scale = jnp.exp(jax.random.uniform(subkeys[1], (1, 1, D), jnp.float32, math.log(0.5), math.log(2.5)))
    values = jnp.clip(jax.random.normal(subkeys[2], (REPLICAS, ROWS, D), jnp.float32), -4.0, 4.0)
    return (values * row_scale * col_scale).astype(jnp.bfloat16)


def projection_draw(key):
    subkeys = jax.random.split(key, 1)
    values = jnp.clip(jax.random.normal(subkeys[0], (D, 3 * D), jnp.float32), -4.0, 4.0) * D ** (-0.5)
    return values


def draw_intra_proj(key, part):
    return projection_draw(jax.random.fold_in(key, 202)).astype(jnp.bfloat16)


def draw_cross_input_weight(key, part):
    return projection_draw(jax.random.fold_in(key, 303)).astype(jnp.bfloat16)


def draw_owner_map(key, part):
    base_key = jax.random.fold_in(key, 404)
    hot_key, order_key, slot_key = jax.random.split(base_key, 3)
    hot = jax.random.randint(hot_key, (REPLICAS, 1, 1), 0, OWNER_DEVICES)
    order_keys = jax.random.split(order_key, REPLICAS * OWNER_DEVICES)
    labels = jax.vmap(lambda subkey: jax.random.permutation(subkey, ROWS_DEV))(order_keys).reshape(REPLICAS, OWNER_DEVICES, ROWS_DEV)
    slot_keys = jax.random.split(slot_key, REPLICAS * OWNER_DEVICES)
    spread_slots = jax.vmap(lambda subkey: jax.random.permutation(subkey, (OWNER_DEVICES - 1) * SEND_LIMIT))(slot_keys).reshape(REPLICAS, OWNER_DEVICES, (OWNER_DEVICES - 1) * SEND_LIMIT)
    index = jnp.clip(labels - SEND_LIMIT, 0, (OWNER_DEVICES - 1) * SEND_LIMIT - 1)
    picked = jnp.take_along_axis(spread_slots, index, axis=2)
    others = (hot + 1 + picked // SEND_LIMIT) % OWNER_DEVICES
    targets = jnp.where(labels < SEND_LIMIT, hot, others)
    return targets.reshape(REPLICAS, ROWS).astype(jnp.int32)


def plant(entries, rng, least, high):
    longest = entries.shape.index(max(entries.shape))
    spots = []
    for shift in (0, 1):
        where = [jax.random.randint(jax.random.fold_in(rng, axis), (), 0, length) for axis, length in enumerate(entries.shape)]
        where[longest] = (where[longest] + shift) % entries.shape[longest]
        spots.append(tuple(where))
    return entries.at[spots[0]].set(least).at[spots[1]].set(high)


def shard_levels(rng, extent, cuts, smallest, high):
    factor_of, own = 1.0, jax.random.fold_in(rng, 6)
    for dim, shards_of in cuts:
        draws = jnp.exp(jax.random.uniform(jax.random.fold_in(own, dim), (shards_of,), jnp.float32, smallest / len(cuts), high / len(cuts)))
        factor_of = factor_of * jnp.repeat(draws, extent[dim] // shards_of).reshape([-1 if axis == dim else 1 for axis in range(len(extent))])
    return factor_of


def bell_draw(rng, dims, scale, most, cuts=(), held_as=jnp.bfloat16):
    loudness = shard_levels(rng, dims, cuts, -0.22, 0.18) if cuts else 1.0
    entries = jax.random.normal(rng, dims, jnp.float32) * scale * loudness
    return jnp.minimum(jnp.maximum(entries, -most), most).astype(held_as)


def setup_inputs(seed: int = 0) -> dict:
    key_list = jax.random.split(jax.random.key(seed), 11)
    return {
        "events": draw_events(jax.random.fold_in(key_list[10], 71), 0),
        "cotangent": bell_draw(key_list[1], (REPLICAS, ROWS, D), 1.0, 6.0, ((0, 8), (1, 32))),
        "intra_gain": jnp.clip(1.0 + 0.15 * jax.random.normal(key_list[2], (D,), jnp.float32), 0.25, 1.75),
        "intra_proj": draw_intra_proj(jax.random.fold_in(key_list[10], 71), 0),
        "intra_out": bell_draw(key_list[4], (D, D), D ** -0.5, 0.25),
        "cross_norm_gain": jnp.clip(1.0 + 0.15 * jax.random.normal(key_list[5], (D,), jnp.float32), 0.25, 1.75),
        "cross_input_weight": draw_cross_input_weight(jax.random.fold_in(key_list[10], 71), 0),
        "cross_output_weight": bell_draw(key_list[7], (D, D), D ** -0.5, 0.25),
        "owner_map": draw_owner_map(jax.random.fold_in(key_list[10], 71), 0),
        "block_lists": plant(jax.random.randint(key_list[9], (REPLICAS, OWNER_DEVICES, NRB, KB), 0, NRB), jax.random.fold_in(key_list[9], 1), 0, NRB - 1).astype(jnp.int32),
    }


EPSILON = 1e-05

def layer_norm(values, scale_factors):
    upcast = values.astype(jnp.float32)
    center = upcast - lax.optimization_barrier(jnp.mean(upcast, axis=-1, keepdims=True))
    spread = lax.optimization_barrier(jnp.mean(center * center, axis=-1, keepdims=True))
    return center * lax.rsqrt(spread + EPSILON) * scale_factors

def split_heads(matrix, block_groups):
    return matrix.reshape(block_groups, EVENTS_PER_BLOCK, HEADS, HEAD_DIM)

def intra_branch(source, scale_factors, input_weight, output_weight):
    row_total, features = source.shape
    block_groups = row_total // EVENTS_PER_BLOCK
    normed = layer_norm(source, scale_factors).astype(jnp.bfloat16)
    packed_rows = jnp.dot(normed, input_weight, preferred_element_type=jnp.float32).astype(jnp.bfloat16)
    queries = split_heads(packed_rows[:, :features], block_groups).astype(jnp.float32)
    key_rows = split_heads(packed_rows[:, features:2 * features], block_groups).astype(jnp.float32)
    value_rows = split_heads(packed_rows[:, 2 * features:], block_groups).astype(jnp.float32)
    scores = jnp.einsum('bqhd,bkhd->bhqk', queries, key_rows) * HEAD_DIM ** (-0.5)
    highest = lax.optimization_barrier(jnp.max(scores, axis=-1, keepdims=True))
    weights = jnp.exp(scores - highest)
    attention = (weights / lax.optimization_barrier(jnp.sum(weights, axis=-1, keepdims=True))).astype(jnp.bfloat16)
    merged_rows = jnp.einsum('bhqk,bkhd->bqhd', attention.astype(jnp.float32), value_rows)
    merged_rows = merged_rows.astype(jnp.bfloat16).reshape(row_total, features)
    branch = jnp.dot(merged_rows, output_weight, preferred_element_type=jnp.float32)
    return (source.astype(jnp.float32) + branch).astype(jnp.bfloat16)

def cross_account_inner(packed_rows, row_presence, block_listing):
    row_total, three_wide = packed_rows.shape
    features = three_wide // 3
    block_groups = row_total // EVENTS_PER_BLOCK
    selected_rows = jnp.concatenate([jnp.arange(block_groups, dtype=jnp.int32)[:, None], block_listing.astype(jnp.int32)], axis=1)
    queries = split_heads(packed_rows[:, :features].astype(jnp.float32), block_groups)
    key_rows = split_heads(packed_rows[:, features:2 * features].astype(jnp.float32), block_groups)[selected_rows]
    key_rows = key_rows.reshape(block_groups, -1, HEADS, HEAD_DIM)
    value_rows = split_heads(packed_rows[:, 2 * features:].astype(jnp.float32), block_groups)[selected_rows]
    value_rows = value_rows.reshape(block_groups, -1, HEADS, HEAD_DIM)
    key_present = row_presence.reshape(block_groups, EVENTS_PER_BLOCK)[selected_rows].reshape(block_groups, -1)
    key_total = key_present.shape[1]
    itself = jnp.arange(key_total, dtype=jnp.int32)[None, :] == jnp.arange(EVENTS_PER_BLOCK, dtype=jnp.int32)[:, None]
    allowed = key_present[:, None, None, :] | itself[None, None, :, :]
    scores = jnp.einsum('bqhd,bkhd->bhqk', queries, key_rows) * HEAD_DIM ** (-0.5)
    scores = jnp.where(allowed, scores, -1e+30)
    highest = lax.optimization_barrier(jnp.max(scores, axis=-1, keepdims=True))
    weights = jnp.where(allowed, jnp.exp(scores - highest), 0.0)
    attention = (weights / lax.optimization_barrier(jnp.sum(weights, axis=-1, keepdims=True))).astype(jnp.bfloat16)
    merged_rows = jnp.einsum('bhqk,bkhd->bqhd', attention.astype(jnp.float32), value_rows)
    return merged_rows.astype(jnp.bfloat16).reshape(row_total, features)

def owner_transfer(landed_rows, landed_cotangent, row_presence, block_listing, scale_factors, input_weight, output_weight):
    normed, norm_pull = jax.vjp(lambda input_operand: layer_norm(input_operand, scale_factors), landed_rows)
    normed_half = normed.astype(jnp.bfloat16)
    packed_rows = jnp.dot(normed_half, input_weight, preferred_element_type=jnp.float32).astype(jnp.bfloat16)
    merged_rows, central_gather = jax.vjp(lambda input_operand: cross_account_inner(input_operand, row_presence, block_listing), packed_rows)
    result = jnp.dot(merged_rows, output_weight, preferred_element_type=jnp.float32).astype(jnp.bfloat16)
    back_mixed = lax.dot_general(landed_cotangent, output_weight, (((1,), (1,)), ((), ())), preferred_element_type=jnp.float32).astype(jnp.bfloat16)
    back_packed = central_gather(back_mixed)[0]
    back_normed = lax.dot_general(back_packed, input_weight, (((1,), (1,)), ((), ())), preferred_element_type=jnp.float32)
    back_rows = norm_pull(back_normed)[0]
    return (result, back_rows, normed_half, back_packed, merged_rows)

def contract(left_part, right_part):
    return lax.dot_general(left_part, right_part, (((0,), (0,)), ((), ())), preferred_element_type=jnp.float32)

def reference(events, cotangent, intra_gain, intra_proj, intra_out, cross_norm_gain, cross_input_weight, cross_output_weight, owner_map, block_lists):

    def replica(running_total, pieces):
        rows_here, upstream, targets, block_listing = pieces
        hidden, intra_pull = jax.vjp(lambda input_operand: intra_branch(input_operand, intra_gain, intra_proj, intra_out), rows_here)
        onehot = (targets[:, None] == jnp.arange(OWNER_DEVICES, dtype=jnp.int32)[None, :]).astype(jnp.int32)
        grouped = onehot.reshape(OWNER_DEVICES, ROWS_DEV, OWNER_DEVICES)
        before = (jnp.cumsum(grouped, axis=1) - grouped).astype(jnp.int32)
        slot_ids = lax.optimization_barrier(jnp.sum(before * grouped, axis=2)).astype(jnp.int32).reshape(ROWS)
        row_counts = lax.optimization_barrier(jnp.sum(grouped, axis=1)).astype(jnp.int32)
        source = jnp.arange(ROWS, dtype=jnp.int32) // ROWS_DEV
        position = (targets * RECEIVE_ROWS + source * SEND_LIMIT + slot_ids).astype(jnp.int32)
        send_buffer = jnp.zeros((OWNER_DEVICES * RECEIVE_ROWS, D), jnp.bfloat16).at[position].set(hidden).reshape(OWNER_DEVICES, RECEIVE_ROWS, D)
        gradient_buffer = jnp.zeros((OWNER_DEVICES * RECEIVE_ROWS, D), jnp.bfloat16).at[position].set(upstream).reshape(OWNER_DEVICES, RECEIVE_ROWS, D)
        row_presence = (jnp.arange(SEND_LIMIT, dtype=jnp.int32)[None, None, :] < row_counts.T[:, :, None]).reshape(OWNER_DEVICES, RECEIVE_ROWS)

        def rows_by_owner(inner, slices):
            landed_rows, landed_cotangent, alive_rows, selected_rows = slices
            result, back_rows, normed_half, back_packed, merged_rows = owner_transfer(landed_rows, landed_cotangent, alive_rows, selected_rows, cross_norm_gain, cross_input_weight, cross_output_weight)
            partial_sum = jnp.concatenate([contract(normed_half, back_packed), contract(merged_rows, landed_cotangent)], axis=1)
            return (inner + partial_sum, (result, back_rows))
        running_total, (output_rows, returned_rows) = lax.scan(rows_by_owner, running_total, (send_buffer, gradient_buffer, row_presence, block_listing))
        result_rows = output_rows.reshape(OWNER_DEVICES * RECEIVE_ROWS, D)[position]
        layer_out = (hidden.astype(jnp.float32) + result_rows.astype(jnp.float32)).astype(jnp.bfloat16)
        return_rows = returned_rows.reshape(OWNER_DEVICES * RECEIVE_ROWS, D)[position]
        grad_hidden = (upstream.astype(jnp.float32) + return_rows.astype(jnp.float32)).astype(jnp.bfloat16)
        grad_rows = intra_pull(grad_hidden)[0]
        return (running_total, (layer_out, grad_rows))
    initial = jnp.zeros((D, 4 * D), jnp.float32)
    summed, (outputs, grads) = lax.scan(replica, initial, (events, cotangent, owner_map, block_lists))
    summed = summed * (REPLICAS * ROWS) ** (-0.5)
    return (outputs, grads, summed[:, :3 * D], summed[:, 3 * D:])
```

```python
import jax
import jax.numpy as jnp
from jax import lax
from jax.sharding import PartitionSpec as P

HEADS = 8
HEAD_DIM = 64
EVENTS_PER_BLOCK = 128


EPSILON = 1e-05


def layer_norm(values, scale_factors):
    upcast = values.astype(jnp.float32)
    center = upcast - jnp.mean(upcast, axis=-1, keepdims=True)
    spread = jnp.mean(center * center, axis=-1, keepdims=True)
    return center * lax.rsqrt(spread + EPSILON) * scale_factors


def split_heads(matrix, block_groups):
    return matrix.reshape(block_groups, EVENTS_PER_BLOCK, HEADS, HEAD_DIM)


def intra_branch(source, scale_factors, input_weight, output_weight):
    row_total, features = source.shape
    block_groups = row_total // EVENTS_PER_BLOCK
    normed = layer_norm(source, scale_factors).astype(jnp.bfloat16)
    packed_rows = jnp.dot(normed, input_weight, preferred_element_type=jnp.float32).astype(
        jnp.bfloat16
    )
    queries = split_heads(packed_rows[:, :features], block_groups).astype(jnp.float32)
    key_rows = split_heads(packed_rows[:, features : 2 * features], block_groups).astype(
        jnp.float32
    )
    value_rows = split_heads(packed_rows[:, 2 * features :], block_groups).astype(jnp.float32)
    scores = jnp.einsum("bqhd,bkhd->bhqk", queries, key_rows) * HEAD_DIM ** (-0.5)
    highest = jnp.max(scores, axis=-1, keepdims=True)
    weights = jnp.exp(scores - highest)
    attention = (weights / jnp.sum(weights, axis=-1, keepdims=True)).astype(jnp.bfloat16)
    merged_rows = jnp.einsum("bhqk,bkhd->bqhd", attention.astype(jnp.float32), value_rows)
    merged_rows = merged_rows.astype(jnp.bfloat16).reshape(row_total, features)
    branch = jnp.dot(merged_rows, output_weight, preferred_element_type=jnp.float32)
    return (source.astype(jnp.float32) + branch).astype(jnp.bfloat16)


def cross_account_inner(packed_rows, row_presence, block_listing):
    row_total, three_wide = packed_rows.shape
    features = three_wide // 3
    block_groups = row_total // EVENTS_PER_BLOCK
    selected_rows = jnp.concatenate(
        [jnp.arange(block_groups, dtype=jnp.int32)[:, None], block_listing], axis=1
    )
    queries = split_heads(packed_rows[:, :features].astype(jnp.float32), block_groups)
    key_rows = split_heads(
        packed_rows[:, features : 2 * features].astype(jnp.float32), block_groups
    )[selected_rows]
    key_rows = key_rows.reshape(block_groups, -1, HEADS, HEAD_DIM)
    value_rows = split_heads(packed_rows[:, 2 * features :].astype(jnp.float32), block_groups)[
        selected_rows
    ]
    value_rows = value_rows.reshape(block_groups, -1, HEADS, HEAD_DIM)
    key_present = row_presence.reshape(block_groups, EVENTS_PER_BLOCK)[selected_rows].reshape(
        block_groups, -1
    )
    key_total = key_present.shape[1]
    itself = (
        jnp.arange(key_total, dtype=jnp.int32)[None, :]
        == jnp.arange(EVENTS_PER_BLOCK, dtype=jnp.int32)[:, None]
    )
    allowed = key_present[:, None, None, :] | itself[None, None, :, :]
    scores = jnp.einsum("bqhd,bkhd->bhqk", queries, key_rows) * HEAD_DIM ** (-0.5)
    scores = jnp.where(allowed, scores, -1e30)
    highest = jnp.max(scores, axis=-1, keepdims=True)
    weights = jnp.where(allowed, jnp.exp(scores - highest), 0.0)
    attention = (weights / jnp.sum(weights, axis=-1, keepdims=True)).astype(jnp.bfloat16)
    merged_rows = jnp.einsum("bhqk,bkhd->bqhd", attention.astype(jnp.float32), value_rows)
    return merged_rows.astype(jnp.bfloat16).reshape(row_total, features)


def owner_transfer(
    landed_rows,
    landed_cotangent,
    row_presence,
    block_listing,
    scale_factors,
    input_weight,
    output_weight,
):
    normed, norm_pull = jax.vjp(
        lambda input_operand: layer_norm(input_operand, scale_factors), landed_rows
    )
    normed_half = normed.astype(jnp.bfloat16)
    packed_rows = jnp.dot(normed_half, input_weight, preferred_element_type=jnp.float32).astype(
        jnp.bfloat16
    )
    merged_rows, central_gather = jax.vjp(
        lambda input_operand: cross_account_inner(input_operand, row_presence, block_listing),
        packed_rows,
    )
    result = jnp.dot(merged_rows, output_weight, preferred_element_type=jnp.float32).astype(
        jnp.bfloat16
    )
    back_mixed = lax.dot_general(
        landed_cotangent,
        output_weight,
        (((1,), (1,)), ((), ())),
        preferred_element_type=jnp.float32,
    ).astype(jnp.bfloat16)
    back_packed = central_gather(back_mixed)[0]
    back_normed = lax.dot_general(
        back_packed, input_weight, (((1,), (1,)), ((), ())), preferred_element_type=jnp.float32
    )
    back_rows = norm_pull(back_normed)[0]
    return (result, back_rows, normed_half, back_packed, merged_rows)


def contract(left_part, right_part):
    return lax.dot_general(
        left_part, right_part, (((0,), (0,)), ((), ())), preferred_element_type=jnp.float32
    )


def reduce_weight_terms(partial, replicas, owners):
    rows, width = partial.shape
    per_owner = rows // owners
    per_device = per_owner // replicas
    terms = partial.astype(jnp.bfloat16).reshape(owners, replicas, per_device, width)
    terms = jnp.swapaxes(terms, 0, 1)
    terms = lax.all_to_all(terms, "dp", 0, 0, tiled=True)
    terms = jnp.sum(terms.astype(jnp.float32), axis=0).astype(jnp.bfloat16)
    terms = lax.all_to_all(terms, "ev", 0, 0, tiled=True)
    piece = jnp.sum(terms.astype(jnp.float32), axis=0)
    copies = jnp.broadcast_to(piece[None], (replicas, per_device, width))
    gathered = lax.all_to_all(copies, "dp", 0, 0, tiled=True)
    return gathered.reshape(per_owner, width)


def on_device(
    events,
    cotangent,
    intra_gain,
    intra_proj,
    intra_out,
    cross_norm_gain,
    cross_input_weight,
    cross_output_weight,
    owner_map,
    block_lists,
):
    rows_here = events[0]
    upstream = cotangent[0]
    local_rows, features = rows_here.shape
    owners = lax.axis_size("ev")
    replicas = lax.axis_size("dp")
    own_index = lax.axis_index("ev")
    row_capacity = 2 * local_rows // owners
    buffer_rows = owners * row_capacity
    hidden, intra_pull = jax.vjp(
        lambda input_operand: intra_branch(input_operand, intra_gain, intra_proj, intra_out),
        rows_here,
    )
    targets = owner_map[0]
    onehot = (targets[:, None] == jnp.arange(owners, dtype=jnp.int32)[None, :]).astype(jnp.int32)
    row_counts = jnp.sum(onehot.reshape(owners, local_rows, owners), axis=1)
    inbound_rows = lax.dynamic_index_in_dim(row_counts, own_index, axis=1, keepdims=False)
    own_onehot = lax.dynamic_slice_in_dim(onehot, own_index * local_rows, local_rows, 0)
    before = jnp.cumsum(own_onehot, axis=0) - own_onehot
    slot_ids = jnp.sum(before * own_onehot, axis=1)
    own_dest = lax.dynamic_slice_in_dim(targets, own_index * local_rows, local_rows, 0)
    position = own_dest * row_capacity + slot_ids
    placement = (
        jnp.arange(buffer_rows, dtype=jnp.int32)[:, None] == position[None, :]
    ).astype(jnp.bfloat16)
    both = jnp.concatenate([hidden, upstream], axis=1)
    outgoing = jnp.dot(placement, both, preferred_element_type=jnp.float32).astype(jnp.bfloat16)
    landed = lax.all_to_all(outgoing, "ev", split_axis=0, concat_axis=0, tiled=True)
    landed_rows = landed[:, :features]
    landed_cotangent = landed[:, features:]
    row_presence = (
        jnp.arange(row_capacity, dtype=jnp.int32)[None, :] < inbound_rows[:, None]
    ).reshape(buffer_rows)
    block_listing = block_lists[0, 0]
    result, back_rows, normed_half, back_packed, merged_rows = owner_transfer(
        landed_rows,
        landed_cotangent,
        row_presence,
        block_listing,
        cross_norm_gain,
        cross_input_weight,
        cross_output_weight,
    )
    going_back = jnp.concatenate([result, back_rows.astype(jnp.bfloat16)], axis=1)
    came_back = lax.all_to_all(going_back, "ev", split_axis=0, concat_axis=0, tiled=True)
    picked = lax.dot_general(
        placement, came_back, (((0,), (0,)), ((), ())), preferred_element_type=jnp.float32
    )
    layer_out = (hidden.astype(jnp.float32) + picked[:, :features]).astype(jnp.bfloat16)
    grad_hidden = (upstream.astype(jnp.float32) + picked[:, features:]).astype(jnp.bfloat16)
    grad_rows = intra_pull(grad_hidden)[0]
    factor = (replicas * owners * local_rows) ** (-0.5)
    partial_sum = jnp.concatenate(
        [contract(normed_half, back_packed), contract(merged_rows, landed_cotangent)], axis=1
    )
    portion = reduce_weight_terms(partial_sum, replicas, owners) * factor
    return (
        layer_out[None],
        grad_rows[None],
        portion[:, : 3 * features],
        portion[:, 3 * features :],
    )


def solution(mesh):
    return jax.shard_map(
        on_device,
        mesh=mesh,
        in_specs=(
            P("dp", "ev", None),
            P("dp", "ev", None),
            P(),
            P(),
            P(),
            P(),
            P(),
            P(),
            P("dp", None),
            P("dp", "ev", None, None),
        ),
        out_specs=(P("dp", "ev", None), P("dp", "ev", None), P("ev", None), P("ev", None)),
        check_vma=False,
    )
```

```python
import jax
import jax.numpy as jnp
from jax import lax
from jax.sharding import PartitionSpec as P

HEADS = 8
HEAD_DIM = 64
EVENTS_PER_BLOCK = 128


EPSILON = 1e-05


def layer_norm(values, scale_factors):
    upcast = values.astype(jnp.float32)
    center = upcast - jnp.mean(upcast, axis=-1, keepdims=True)
    spread = jnp.mean(center * center, axis=-1, keepdims=True)
    return center * lax.rsqrt(spread + EPSILON) * scale_factors


def split_heads(matrix, block_groups):
    return matrix.reshape(block_groups, EVENTS_PER_BLOCK, HEADS, HEAD_DIM)


def intra_branch(source, scale_factors, input_weight, output_weight):
    row_total, features = source.shape
    block_groups = row_total // EVENTS_PER_BLOCK
    normed = layer_norm(source, scale_factors).astype(jnp.bfloat16)
    packed_rows = jnp.dot(normed, input_weight, preferred_element_type=jnp.float32).astype(
        jnp.bfloat16
    )
    queries = split_heads(packed_rows[:, :features], block_groups).astype(jnp.float32)
    key_rows = split_heads(packed_rows[:, features : 2 * features], block_groups).astype(
        jnp.float32
    )
    value_rows = split_heads(packed_rows[:, 2 * features :], block_groups).astype(jnp.float32)
    scores = jnp.einsum("bqhd,bkhd->bhqk", queries, key_rows) * HEAD_DIM ** (-0.5)
    highest = jnp.max(scores, axis=-1, keepdims=True)
    weights = jnp.exp(scores - highest)
    attention = (weights / jnp.sum(weights, axis=-1, keepdims=True)).astype(jnp.bfloat16)
    merged_rows = jnp.einsum("bhqk,bkhd->bqhd", attention.astype(jnp.float32), value_rows)
    merged_rows = merged_rows.astype(jnp.bfloat16).reshape(row_total, features)
    branch = jnp.dot(merged_rows, output_weight, preferred_element_type=jnp.float32)
    return (source.astype(jnp.float32) + branch).astype(jnp.bfloat16)


def pick_blocks(blocks, chosen):
    picked = blocks[0]
    for index in range(1, blocks.shape[0]):
        picked = jnp.where(chosen == index, blocks[index], picked)
    return picked


def cross_account_inner(packed_rows, row_presence, block_listing):
    row_total, three_wide = packed_rows.shape
    features = three_wide // 3
    block_groups = row_total // EVENTS_PER_BLOCK
    selected_rows = jnp.concatenate(
        [jnp.arange(block_groups, dtype=jnp.int32)[:, None], block_listing], axis=1
    )
    segments = selected_rows.shape[1]
    chosen = selected_rows[:, :, None, None, None]
    queries = split_heads(packed_rows[:, :features].astype(jnp.float32), block_groups)
    key_blocks = split_heads(
        packed_rows[:, features : 2 * features].astype(jnp.float32), block_groups
    )
    key_rows = pick_blocks(key_blocks[:, None], chosen)
    key_rows = key_rows.reshape(block_groups, segments * EVENTS_PER_BLOCK, HEADS, HEAD_DIM)
    value_blocks = split_heads(packed_rows[:, 2 * features :].astype(jnp.float32), block_groups)
    value_rows = pick_blocks(value_blocks[:, None], chosen)
    value_rows = value_rows.reshape(block_groups, segments * EVENTS_PER_BLOCK, HEADS, HEAD_DIM)
    presence_blocks = row_presence.reshape(block_groups, EVENTS_PER_BLOCK)
    key_present = pick_blocks(presence_blocks[:, None], selected_rows[:, :, None])
    key_present = key_present.reshape(block_groups, -1)
    key_total = key_present.shape[1]
    itself = (
        jnp.arange(key_total, dtype=jnp.int32)[None, :]
        == jnp.arange(EVENTS_PER_BLOCK, dtype=jnp.int32)[:, None]
    )
    allowed = key_present[:, None, None, :] | itself[None, None, :, :]
    scores = jnp.einsum("bqhd,bkhd->bhqk", queries, key_rows) * HEAD_DIM ** (-0.5)
    scores = jnp.where(allowed, scores, -1e30)
    highest = jnp.max(scores, axis=-1, keepdims=True)
    weights = jnp.where(allowed, jnp.exp(scores - highest), 0.0)
    attention = (weights / jnp.sum(weights, axis=-1, keepdims=True)).astype(jnp.bfloat16)
    merged_rows = jnp.einsum("bhqk,bkhd->bqhd", attention.astype(jnp.float32), value_rows)
    return merged_rows.astype(jnp.bfloat16).reshape(row_total, features)


def owner_transfer(
    landed_rows,
    landed_cotangent,
    row_presence,
    block_listing,
    scale_factors,
    input_weight,
    output_weight,
):
    normed, norm_pull = jax.vjp(
        lambda input_operand: layer_norm(input_operand, scale_factors), landed_rows
    )
    normed_half = normed.astype(jnp.bfloat16)
    packed_rows = jnp.dot(normed_half, input_weight, preferred_element_type=jnp.float32).astype(
        jnp.bfloat16
    )
    merged_rows, central_gather = jax.vjp(
        lambda input_operand: cross_account_inner(input_operand, row_presence, block_listing),
        packed_rows,
    )
    result = jnp.dot(merged_rows, output_weight, preferred_element_type=jnp.float32).astype(
        jnp.bfloat16
    )
    back_mixed = lax.dot_general(
        landed_cotangent,
        output_weight,
        (((1,), (1,)), ((), ())),
        preferred_element_type=jnp.float32,
    ).astype(jnp.bfloat16)
    back_packed = central_gather(back_mixed)[0]
    back_normed = lax.dot_general(
        back_packed, input_weight, (((1,), (1,)), ((), ())), preferred_element_type=jnp.float32
    )
    back_rows = norm_pull(back_normed)[0]
    return (result, back_rows, normed_half, back_packed, merged_rows)


def contract(left_part, right_part):
    return lax.dot_general(
        left_part, right_part, (((0,), (0,)), ((), ())), preferred_element_type=jnp.float32
    )


def reduce_weight_terms(partial, replicas, owners):
    rows, width = partial.shape
    per_owner = rows // owners
    per_device = per_owner // replicas
    terms = partial.astype(jnp.bfloat16).reshape(owners, replicas, per_device, width)
    terms = jnp.swapaxes(terms, 0, 1)
    terms = lax.all_to_all(terms, "dp", 0, 0, tiled=True)
    terms = jnp.sum(terms.astype(jnp.float32), axis=0).astype(jnp.bfloat16)
    terms = lax.all_to_all(terms, "ev", 0, 0, tiled=True)
    piece = jnp.sum(terms.astype(jnp.float32), axis=0)
    copies = jnp.broadcast_to(piece[None], (replicas, per_device, width))
    gathered = lax.all_to_all(copies, "dp", 0, 0, tiled=True)
    return gathered.reshape(per_owner, width)


def on_device(
    events,
    cotangent,
    intra_gain,
    intra_proj,
    intra_out,
    cross_norm_gain,
    cross_input_weight,
    cross_output_weight,
    owner_map,
    block_lists,
):
    rows_here = events[0]
    upstream = cotangent[0]
    local_rows, features = rows_here.shape
    owners = lax.axis_size("ev")
    replicas = lax.axis_size("dp")
    own_index = lax.axis_index("ev")
    row_capacity = 2 * local_rows // owners
    buffer_rows = owners * row_capacity
    hidden, intra_pull = jax.vjp(
        lambda input_operand: intra_branch(input_operand, intra_gain, intra_proj, intra_out),
        rows_here,
    )
    targets = owner_map[0]
    onehot = (targets[:, None] == jnp.arange(owners, dtype=jnp.int32)[None, :]).astype(jnp.int32)
    row_counts = jnp.sum(onehot.reshape(owners, local_rows, owners), axis=1)
    inbound_rows = lax.dynamic_index_in_dim(row_counts, own_index, axis=1, keepdims=False)
    own_onehot = lax.dynamic_slice_in_dim(onehot, own_index * local_rows, local_rows, 0)
    before = jnp.cumsum(own_onehot, axis=0) - own_onehot
    slot_ids = jnp.sum(before * own_onehot, axis=1)
    own_dest = lax.dynamic_slice_in_dim(targets, own_index * local_rows, local_rows, 0)
    position = own_dest * row_capacity + slot_ids
    placement = (
        jnp.arange(buffer_rows, dtype=jnp.int32)[:, None] == position[None, :]
    ).astype(jnp.bfloat16)
    both = jnp.concatenate([hidden, upstream], axis=1)
    outgoing = jnp.dot(placement, both, preferred_element_type=jnp.float32).astype(jnp.bfloat16)
    landed = lax.all_to_all(outgoing, "ev", split_axis=0, concat_axis=0, tiled=True)
    landed_rows = landed[:, :features]
    landed_cotangent = landed[:, features:]
    row_presence = (
        jnp.arange(row_capacity, dtype=jnp.int32)[None, :] < inbound_rows[:, None]
    ).reshape(buffer_rows)
    block_listing = block_lists[0, 0]
    result, back_rows, normed_half, back_packed, merged_rows = owner_transfer(
        landed_rows,
        landed_cotangent,
        row_presence,
        block_listing,
        cross_norm_gain,
        cross_input_weight,
        cross_output_weight,
    )
    going_back = jnp.concatenate([result, back_rows.astype(jnp.bfloat16)], axis=1)
    came_back = lax.all_to_all(going_back, "ev", split_axis=0, concat_axis=0, tiled=True)
    picked = lax.dot_general(
        placement, came_back, (((0,), (0,)), ((), ())), preferred_element_type=jnp.float32
    )
    layer_out = (hidden.astype(jnp.float32) + picked[:, :features]).astype(jnp.bfloat16)
    grad_hidden = (upstream.astype(jnp.float32) + picked[:, features:]).astype(jnp.bfloat16)
    grad_rows = intra_pull(grad_hidden)[0]
    factor = (replicas * owners * local_rows) ** (-0.5)
    partial_sum = jnp.concatenate(
        [contract(normed_half, back_packed), contract(merged_rows, landed_cotangent)], axis=1
    )
    portion = reduce_weight_terms(partial_sum, replicas, owners) * factor
    return (
        layer_out[None],
        grad_rows[None],
        portion[:, : 3 * features],
        portion[:, 3 * features :],
    )


def solution(mesh):
    return jax.shard_map(
        on_device,
        mesh=mesh,
        in_specs=(
            P("dp", "ev", None),
            P("dp", "ev", None),
            P(),
            P(),
            P(),
            P(),
            P(),
            P(),
            P("dp", None),
            P("dp", "ev", None, None),
        ),
        out_specs=(P("dp", "ev", None), P("dp", "ev", None), P("ev", None), P("ev", None)),
        check_vma=False,
    )
```

```python
import jax
import jax.numpy as jnp
from jax import lax
from jax.sharding import PartitionSpec as P

HEADS = 8
HEAD_DIM = 64
EVENTS_PER_BLOCK = 128


EPSILON = 1e-05


def layer_norm(values, scale_factors):
    upcast = values.astype(jnp.float32)
    center = upcast - jnp.mean(upcast, axis=-1, keepdims=True)
    spread = jnp.mean(center * center, axis=-1, keepdims=True)
    return center * lax.rsqrt(spread + EPSILON) * scale_factors


def split_heads(matrix, block_groups):
    return matrix.reshape(block_groups, EVENTS_PER_BLOCK, HEADS, HEAD_DIM)


def intra_branch(source, scale_factors, input_weight, output_weight):
    row_total, features = source.shape
    block_groups = row_total // EVENTS_PER_BLOCK
    normed = layer_norm(source, scale_factors).astype(jnp.bfloat16)
    packed_rows = jnp.dot(normed, input_weight, preferred_element_type=jnp.float32).astype(
        jnp.bfloat16
    )
    queries = split_heads(packed_rows[:, :features], block_groups).astype(jnp.float32)
    key_rows = split_heads(packed_rows[:, features : 2 * features], block_groups).astype(
        jnp.float32
    )
    value_rows = split_heads(packed_rows[:, 2 * features :], block_groups).astype(jnp.float32)
    scores = jnp.einsum("bqhd,bkhd->bhqk", queries, key_rows) * HEAD_DIM ** (-0.5)
    highest = jnp.max(scores, axis=-1, keepdims=True)
    weights = jnp.exp(scores - highest)
    attention = (weights / jnp.sum(weights, axis=-1, keepdims=True)).astype(jnp.bfloat16)
    merged_rows = jnp.einsum("bhqk,bkhd->bqhd", attention.astype(jnp.float32), value_rows)
    merged_rows = merged_rows.astype(jnp.bfloat16).reshape(row_total, features)
    branch = jnp.dot(merged_rows, output_weight, preferred_element_type=jnp.float32)
    return (source.astype(jnp.float32) + branch).astype(jnp.bfloat16)


def pick_block(blocks, chosen):
    picked = blocks[0]
    for index in range(1, blocks.shape[0]):
        picked = jnp.where(chosen == index, blocks[index], picked)
    return picked


def gather_segments(blocks, selected_rows):
    block_groups, segments = selected_rows.shape
    return jnp.stack(
        [
            jnp.concatenate(
                [pick_block(blocks, selected_rows[group, segment]) for segment in range(segments)],
                axis=0,
            )
            for group in range(block_groups)
        ],
        axis=0,
    )


def cross_account_inner(packed_rows, row_presence, block_listing):
    row_total, three_wide = packed_rows.shape
    features = three_wide // 3
    block_groups = row_total // EVENTS_PER_BLOCK
    selected_rows = jnp.concatenate(
        [jnp.arange(block_groups, dtype=jnp.int32)[:, None], block_listing], axis=1
    )
    queries = split_heads(packed_rows[:, :features].astype(jnp.float32), block_groups)
    key_blocks = split_heads(
        packed_rows[:, features : 2 * features].astype(jnp.float32), block_groups
    )
    key_rows = gather_segments(key_blocks, selected_rows)
    value_blocks = split_heads(packed_rows[:, 2 * features :].astype(jnp.float32), block_groups)
    value_rows = gather_segments(value_blocks, selected_rows)
    presence_blocks = row_presence.reshape(block_groups, EVENTS_PER_BLOCK)
    key_present = gather_segments(presence_blocks, selected_rows)
    key_total = key_present.shape[1]
    itself = (
        jnp.arange(key_total, dtype=jnp.int32)[None, :]
        == jnp.arange(EVENTS_PER_BLOCK, dtype=jnp.int32)[:, None]
    )
    allowed = key_present[:, None, None, :] | itself[None, None, :, :]
    scores = jnp.einsum("bqhd,bkhd->bhqk", queries, key_rows) * HEAD_DIM ** (-0.5)
    scores = jnp.where(allowed, scores, -1e30)
    highest = jnp.max(scores, axis=-1, keepdims=True)
    weights = jnp.where(allowed, jnp.exp(scores - highest), 0.0)
    attention = (weights / jnp.sum(weights, axis=-1, keepdims=True)).astype(jnp.bfloat16)
    merged_rows = jnp.einsum("bhqk,bkhd->bqhd", attention.astype(jnp.float32), value_rows)
    return merged_rows.astype(jnp.bfloat16).reshape(row_total, features)


def owner_transfer(
    landed_rows,
    landed_cotangent,
    row_presence,
    block_listing,
    scale_factors,
    input_weight,
    output_weight,
):
    normed, norm_pull = jax.vjp(
        lambda input_operand: layer_norm(input_operand, scale_factors), landed_rows
    )
    normed_half = normed.astype(jnp.bfloat16)
    packed_rows = jnp.dot(normed_half, input_weight, preferred_element_type=jnp.float32).astype(
        jnp.bfloat16
    )
    merged_rows, central_gather = jax.vjp(
        lambda input_operand: cross_account_inner(input_operand, row_presence, block_listing),
        packed_rows,
    )
    result = jnp.dot(merged_rows, output_weight, preferred_element_type=jnp.float32).astype(
        jnp.bfloat16
    )
    back_mixed = lax.dot_general(
        landed_cotangent,
        output_weight,
        (((1,), (1,)), ((), ())),
        preferred_element_type=jnp.float32,
    ).astype(jnp.bfloat16)
    back_packed = central_gather(back_mixed)[0]
    back_normed = lax.dot_general(
        back_packed, input_weight, (((1,), (1,)), ((), ())), preferred_element_type=jnp.float32
    )
    back_rows = norm_pull(back_normed)[0]
    return (result, back_rows, normed_half, back_packed, merged_rows)


def contract(left_part, right_part):
    return lax.dot_general(
        left_part, right_part, (((0,), (0,)), ((), ())), preferred_element_type=jnp.float32
    )


def reduce_weight_terms(partial, replicas, owners):
    rows, width = partial.shape
    per_owner = rows // owners
    per_device = per_owner // replicas
    terms = partial.astype(jnp.bfloat16).reshape(owners, replicas, per_device, width)
    terms = jnp.swapaxes(terms, 0, 1)
    terms = lax.all_to_all(terms, "dp", 0, 0, tiled=True)
    terms = jnp.sum(terms.astype(jnp.float32), axis=0).astype(jnp.bfloat16)
    terms = lax.all_to_all(terms, "ev", 0, 0, tiled=True)
    piece = jnp.sum(terms.astype(jnp.float32), axis=0)
    copies = jnp.broadcast_to(piece[None], (replicas, per_device, width))
    gathered = lax.all_to_all(copies, "dp", 0, 0, tiled=True)
    return gathered.reshape(per_owner, width)


def on_device(
    events,
    cotangent,
    intra_gain,
    intra_proj,
    intra_out,
    cross_norm_gain,
    cross_input_weight,
    cross_output_weight,
    owner_map,
    block_lists,
):
    rows_here = events[0]
    upstream = cotangent[0]
    local_rows, features = rows_here.shape
    owners = lax.axis_size("ev")
    replicas = lax.axis_size("dp")
    own_index = lax.axis_index("ev")
    row_capacity = 2 * local_rows // owners
    buffer_rows = owners * row_capacity
    hidden, intra_pull = jax.vjp(
        lambda input_operand: intra_branch(input_operand, intra_gain, intra_proj, intra_out),
        rows_here,
    )
    targets = owner_map[0]
    onehot = (targets[:, None] == jnp.arange(owners, dtype=jnp.int32)[None, :]).astype(jnp.int32)
    row_counts = jnp.sum(onehot.reshape(owners, local_rows, owners), axis=1)
    inbound_rows = lax.dynamic_index_in_dim(row_counts, own_index, axis=1, keepdims=False)
    own_onehot = lax.dynamic_slice_in_dim(onehot, own_index * local_rows, local_rows, 0)
    before = jnp.cumsum(own_onehot, axis=0) - own_onehot
    slot_ids = jnp.sum(before * own_onehot, axis=1)
    own_dest = lax.dynamic_slice_in_dim(targets, own_index * local_rows, local_rows, 0)
    position = own_dest * row_capacity + slot_ids
    placement = (
        jnp.arange(buffer_rows, dtype=jnp.int32)[:, None] == position[None, :]
    ).astype(jnp.bfloat16)
    both = jnp.concatenate([hidden, upstream], axis=1)
    outgoing = jnp.dot(placement, both, preferred_element_type=jnp.float32).astype(jnp.bfloat16)
    landed = lax.all_to_all(outgoing, "ev", split_axis=0, concat_axis=0, tiled=True)
    landed_rows = landed[:, :features]
    landed_cotangent = landed[:, features:]
    row_presence = (
        jnp.arange(row_capacity, dtype=jnp.int32)[None, :] < inbound_rows[:, None]
    ).reshape(buffer_rows)
    block_listing = block_lists[0, 0]
    result, back_rows, normed_half, back_packed, merged_rows = owner_transfer(
        landed_rows,
        landed_cotangent,
        row_presence,
        block_listing,
        cross_norm_gain,
        cross_input_weight,
        cross_output_weight,
    )
    going_back = jnp.concatenate([result, back_rows.astype(jnp.bfloat16)], axis=1)
    came_back = lax.all_to_all(going_back, "ev", split_axis=0, concat_axis=0, tiled=True)
    picked = lax.dot_general(
        placement, came_back, (((0,), (0,)), ((), ())), preferred_element_type=jnp.float32
    )
    layer_out = (hidden.astype(jnp.float32) + picked[:, :features]).astype(jnp.bfloat16)
    grad_hidden = (upstream.astype(jnp.float32) + picked[:, features:]).astype(jnp.bfloat16)
    grad_rows = intra_pull(grad_hidden)[0]
    factor = (replicas * owners * local_rows) ** (-0.5)
    partial_sum = jnp.concatenate(
        [contract(normed_half, back_packed), contract(merged_rows, landed_cotangent)], axis=1
    )
    portion = reduce_weight_terms(partial_sum, replicas, owners) * factor
    return (
        layer_out[None],
        grad_rows[None],
        portion[:, : 3 * features],
        portion[:, 3 * features :],
    )


def solution(mesh):
    return jax.shard_map(
        on_device,
        mesh=mesh,
        in_specs=(
            P("dp", "ev", None),
            P("dp", "ev", None),
            P(),
            P(),
            P(),
            P(),
            P(),
            P(),
            P("dp", None),
            P("dp", "ev", None, None),
        ),
        out_specs=(P("dp", "ev", None), P("dp", "ev", None), P("ev", None), P("ev", None)),
        check_vma=False,
    )
```

```python
import jax
import jax.numpy as jnp
from jax import lax
from jax.sharding import PartitionSpec as P

HEADS = 8
HEAD_DIM = 64
EVENTS_PER_BLOCK = 128


EPSILON = 1e-05


def layer_norm(values, scale_factors):
    upcast = values.astype(jnp.float32)
    center = upcast - jnp.mean(upcast, axis=-1, keepdims=True)
    spread = jnp.mean(center * center, axis=-1, keepdims=True)
    return center * lax.rsqrt(spread + EPSILON) * scale_factors


def split_heads(matrix, block_groups):
    return matrix.reshape(block_groups, EVENTS_PER_BLOCK, HEADS, HEAD_DIM)


def heads_first(packed_rows, block_groups):
    parts = packed_rows.reshape(block_groups, EVENTS_PER_BLOCK, 3, HEADS, HEAD_DIM)
    return jnp.transpose(parts, (2, 0, 3, 1, 4)).astype(jnp.float32)


def rows_first(merged, row_total):
    return jnp.transpose(merged, (0, 2, 1, 3)).astype(jnp.bfloat16).reshape(row_total, -1)


def intra_branch(source, scale_factors, input_weight, output_weight):
    row_total, features = source.shape
    block_groups = row_total // EVENTS_PER_BLOCK
    normed = layer_norm(source, scale_factors).astype(jnp.bfloat16)
    packed_rows = jnp.dot(normed, input_weight, preferred_element_type=jnp.float32).astype(
        jnp.bfloat16
    )
    parts = heads_first(packed_rows, block_groups)
    queries, key_rows, value_rows = parts[0], parts[1], parts[2]
    scores = jnp.einsum("bhqd,bhkd->bhqk", queries, key_rows) * HEAD_DIM ** (-0.5)
    highest = jnp.max(scores, axis=-1, keepdims=True)
    weights = jnp.exp(scores - highest)
    attention = (weights / jnp.sum(weights, axis=-1, keepdims=True)).astype(jnp.bfloat16)
    merged_rows = jnp.einsum("bhqk,bhkd->bhqd", attention.astype(jnp.float32), value_rows)
    merged_rows = rows_first(merged_rows, row_total)
    branch = jnp.dot(merged_rows, output_weight, preferred_element_type=jnp.float32)
    return (source.astype(jnp.float32) + branch).astype(jnp.bfloat16)


def pick_block(blocks, chosen):
    picked = blocks[0]
    for index in range(1, blocks.shape[0]):
        picked = jnp.where(chosen == index, blocks[index], picked)
    return picked


def gather_segments(blocks, selected_rows, axis):
    block_groups, segments = selected_rows.shape
    return jnp.stack(
        [
            jnp.concatenate(
                [pick_block(blocks, selected_rows[group, segment]) for segment in range(segments)],
                axis=axis,
            )
            for group in range(block_groups)
        ],
        axis=0,
    )


def cross_account_inner(packed_rows, row_presence, block_listing):
    row_total, three_wide = packed_rows.shape
    block_groups = row_total // EVENTS_PER_BLOCK
    selected_rows = jnp.concatenate(
        [jnp.arange(block_groups, dtype=jnp.int32)[:, None], block_listing], axis=1
    )
    parts = heads_first(packed_rows, block_groups)
    queries = parts[0]
    key_rows = gather_segments(parts[1], selected_rows, 1)
    value_rows = gather_segments(parts[2], selected_rows, 1)
    presence_blocks = row_presence.reshape(block_groups, EVENTS_PER_BLOCK)
    key_present = gather_segments(presence_blocks, selected_rows, 0)
    key_total = key_present.shape[1]
    itself = (
        jnp.arange(key_total, dtype=jnp.int32)[None, :]
        == jnp.arange(EVENTS_PER_BLOCK, dtype=jnp.int32)[:, None]
    )
    allowed = key_present[:, None, None, :] | itself[None, None, :, :]
    scores = jnp.einsum("bhqd,bhkd->bhqk", queries, key_rows) * HEAD_DIM ** (-0.5)
    scores = jnp.where(allowed, scores, -1e30)
    highest = jnp.max(scores, axis=-1, keepdims=True)
    weights = jnp.where(allowed, jnp.exp(scores - highest), 0.0)
    attention = (weights / jnp.sum(weights, axis=-1, keepdims=True)).astype(jnp.bfloat16)
    merged_rows = jnp.einsum("bhqk,bhkd->bhqd", attention.astype(jnp.float32), value_rows)
    return rows_first(merged_rows, row_total)


def owner_transfer(
    landed_rows,
    landed_cotangent,
    row_presence,
    block_listing,
    scale_factors,
    input_weight,
    output_weight,
):
    normed, norm_pull = jax.vjp(
        lambda input_operand: layer_norm(input_operand, scale_factors), landed_rows
    )
    normed_half = normed.astype(jnp.bfloat16)
    packed_rows = jnp.dot(normed_half, input_weight, preferred_element_type=jnp.float32).astype(
        jnp.bfloat16
    )
    merged_rows, central_gather = jax.vjp(
        lambda input_operand: cross_account_inner(input_operand, row_presence, block_listing),
        packed_rows,
    )
    result = jnp.dot(merged_rows, output_weight, preferred_element_type=jnp.float32).astype(
        jnp.bfloat16
    )
    back_mixed = lax.dot_general(
        landed_cotangent,
        output_weight,
        (((1,), (1,)), ((), ())),
        preferred_element_type=jnp.float32,
    ).astype(jnp.bfloat16)
    back_packed = central_gather(back_mixed)[0]
    back_normed = lax.dot_general(
        back_packed, input_weight, (((1,), (1,)), ((), ())), preferred_element_type=jnp.float32
    )
    back_rows = norm_pull(back_normed)[0]
    return (result, back_rows, normed_half, back_packed, merged_rows)


def contract(left_part, right_part):
    return lax.dot_general(
        left_part, right_part, (((0,), (0,)), ((), ())), preferred_element_type=jnp.float32
    )


def reduce_weight_terms(partial, replicas, owners):
    rows, width = partial.shape
    per_owner = rows // owners
    per_device = per_owner // replicas
    terms = partial.astype(jnp.bfloat16).reshape(owners, replicas, per_device, width)
    terms = jnp.swapaxes(terms, 0, 1)
    terms = lax.all_to_all(terms, "dp", 0, 0, tiled=True)
    terms = jnp.sum(terms.astype(jnp.float32), axis=0).astype(jnp.bfloat16)
    terms = lax.all_to_all(terms, "ev", 0, 0, tiled=True)
    piece = jnp.sum(terms.astype(jnp.float32), axis=0)
    copies = jnp.broadcast_to(piece[None], (replicas, per_device, width))
    gathered = lax.all_to_all(copies, "dp", 0, 0, tiled=True)
    return gathered.reshape(per_owner, width)


def on_device(
    events,
    cotangent,
    intra_gain,
    intra_proj,
    intra_out,
    cross_norm_gain,
    cross_input_weight,
    cross_output_weight,
    owner_map,
    block_lists,
):
    rows_here = events[0]
    upstream = cotangent[0]
    local_rows, features = rows_here.shape
    owners = lax.axis_size("ev")
    replicas = lax.axis_size("dp")
    own_index = lax.axis_index("ev")
    row_capacity = 2 * local_rows // owners
    buffer_rows = owners * row_capacity
    hidden, intra_pull = jax.vjp(
        lambda input_operand: intra_branch(input_operand, intra_gain, intra_proj, intra_out),
        rows_here,
    )
    targets = owner_map[0]
    onehot = (targets[:, None] == jnp.arange(owners, dtype=jnp.int32)[None, :]).astype(jnp.int32)
    row_counts = jnp.sum(onehot.reshape(owners, local_rows, owners), axis=1)
    inbound_rows = lax.dynamic_index_in_dim(row_counts, own_index, axis=1, keepdims=False)
    own_onehot = lax.dynamic_slice_in_dim(onehot, own_index * local_rows, local_rows, 0)
    before = jnp.cumsum(own_onehot, axis=0) - own_onehot
    slot_ids = jnp.sum(before * own_onehot, axis=1)
    own_dest = lax.dynamic_slice_in_dim(targets, own_index * local_rows, local_rows, 0)
    position = own_dest * row_capacity + slot_ids
    placement = (
        jnp.arange(buffer_rows, dtype=jnp.int32)[:, None] == position[None, :]
    ).astype(jnp.bfloat16)
    both = jnp.concatenate([hidden, upstream], axis=1)
    outgoing = jnp.dot(placement, both, preferred_element_type=jnp.float32).astype(jnp.bfloat16)
    landed = lax.all_to_all(outgoing, "ev", split_axis=0, concat_axis=0, tiled=True)
    landed_rows = landed[:, :features]
    landed_cotangent = landed[:, features:]
    row_presence = (
        jnp.arange(row_capacity, dtype=jnp.int32)[None, :] < inbound_rows[:, None]
    ).reshape(buffer_rows)
    block_listing = block_lists[0, 0]
    result, back_rows, normed_half, back_packed, merged_rows = owner_transfer(
        landed_rows,
        landed_cotangent,
        row_presence,
        block_listing,
        cross_norm_gain,
        cross_input_weight,
        cross_output_weight,
    )
    going_back = jnp.concatenate([result, back_rows.astype(jnp.bfloat16)], axis=1)
    came_back = lax.all_to_all(going_back, "ev", split_axis=0, concat_axis=0, tiled=True)
    picked = lax.dot_general(
        placement, came_back, (((0,), (0,)), ((), ())), preferred_element_type=jnp.float32
    )
    layer_out = (hidden.astype(jnp.float32) + picked[:, :features]).astype(jnp.bfloat16)
    grad_hidden = (upstream.astype(jnp.float32) + picked[:, features:]).astype(jnp.bfloat16)
    grad_rows = intra_pull(grad_hidden)[0]
    factor = (replicas * owners * local_rows) ** (-0.5)
    partial_sum = jnp.concatenate(
        [contract(normed_half, back_packed), contract(merged_rows, landed_cotangent)], axis=1
    )
    portion = reduce_weight_terms(partial_sum, replicas, owners) * factor
    return (
        layer_out[None],
        grad_rows[None],
        portion[:, : 3 * features],
        portion[:, 3 * features :],
    )


def solution(mesh):
    return jax.shard_map(
        on_device,
        mesh=mesh,
        in_specs=(
            P("dp", "ev", None),
            P("dp", "ev", None),
            P(),
            P(),
            P(),
            P(),
            P(),
            P(),
            P("dp", None),
            P("dp", "ev", None, None),
        ),
        out_specs=(P("dp", "ev", None), P("dp", "ev", None), P("ev", None), P("ev", None)),
        check_vma=False,
    )
```

```python
import jax
import jax.numpy as jnp
from jax import lax
from jax.sharding import PartitionSpec as P

HEADS = 8
HEAD_DIM = 64
EVENTS_PER_BLOCK = 128


EPSILON = 1e-05


def layer_norm(values, scale_factors):
    upcast = values.astype(jnp.float32)
    center = upcast - jnp.mean(upcast, axis=-1, keepdims=True)
    spread = jnp.mean(center * center, axis=-1, keepdims=True)
    return center * lax.rsqrt(spread + EPSILON) * scale_factors


def split_heads(matrix, block_groups):
    return matrix.reshape(block_groups, EVENTS_PER_BLOCK, HEADS, HEAD_DIM)


def heads_first(packed_rows, block_groups):
    parts = packed_rows.reshape(block_groups, EVENTS_PER_BLOCK, 3, HEADS, HEAD_DIM)
    return jnp.transpose(parts, (2, 0, 3, 1, 4)).astype(jnp.float32)


def rows_first(merged, row_total):
    return jnp.transpose(merged, (0, 2, 1, 3)).astype(jnp.bfloat16).reshape(row_total, -1)


def intra_branch(source, scale_factors, input_weight, output_weight):
    row_total, features = source.shape
    block_groups = row_total // EVENTS_PER_BLOCK
    normed = layer_norm(source, scale_factors).astype(jnp.bfloat16)
    packed_rows = jnp.dot(normed, input_weight, preferred_element_type=jnp.float32).astype(
        jnp.bfloat16
    )
    parts = heads_first(packed_rows, block_groups)
    queries, key_rows, value_rows = parts[0], parts[1], parts[2]
    scores = jnp.einsum("bhqd,bhkd->bhqk", queries, key_rows) * HEAD_DIM ** (-0.5)
    highest = jnp.max(scores, axis=-1, keepdims=True)
    weights = jnp.exp(scores - highest)
    attention = (weights / jnp.sum(weights, axis=-1, keepdims=True)).astype(jnp.bfloat16)
    merged_rows = jnp.einsum("bhqk,bhkd->bhqd", attention.astype(jnp.float32), value_rows)
    merged_rows = rows_first(merged_rows, row_total)
    branch = jnp.dot(merged_rows, output_weight, preferred_element_type=jnp.float32)
    return (source.astype(jnp.float32) + branch).astype(jnp.bfloat16)


def pick_block(blocks, chosen):
    picked = blocks[0]
    for index in range(1, blocks.shape[0]):
        picked = jnp.where(chosen == index, blocks[index], picked)
    return picked


def gather_segments(blocks, selected_rows, axis):
    block_groups, segments = selected_rows.shape
    return jnp.stack(
        [
            jnp.concatenate(
                [pick_block(blocks, selected_rows[group, segment]) for segment in range(segments)],
                axis=axis,
            )
            for group in range(block_groups)
        ],
        axis=0,
    )


def cross_account_inner(packed_rows, row_presence, block_listing):
    row_total, three_wide = packed_rows.shape
    block_groups = row_total // EVENTS_PER_BLOCK
    selected_rows = jnp.concatenate(
        [jnp.arange(block_groups, dtype=jnp.int32)[:, None], block_listing], axis=1
    )
    parts = heads_first(packed_rows, block_groups)
    queries = parts[0]
    key_rows = gather_segments(parts[1], selected_rows, 1)
    value_rows = gather_segments(parts[2], selected_rows, 1)
    presence_blocks = row_presence.reshape(block_groups, EVENTS_PER_BLOCK)
    key_present = gather_segments(presence_blocks, selected_rows, 0)
    key_total = key_present.shape[1]
    itself = (
        jnp.arange(key_total, dtype=jnp.int32)[None, :]
        == jnp.arange(EVENTS_PER_BLOCK, dtype=jnp.int32)[:, None]
    )
    allowed = key_present[:, None, None, :] | itself[None, None, :, :]
    scores = jnp.einsum("bhqd,bhkd->bhqk", queries, key_rows) * HEAD_DIM ** (-0.5)
    scores = jnp.where(allowed, scores, -1e30)
    highest = jnp.max(scores, axis=-1, keepdims=True)
    weights = jnp.where(allowed, jnp.exp(scores - highest), 0.0)
    attention = (weights / jnp.sum(weights, axis=-1, keepdims=True)).astype(jnp.bfloat16)
    merged_rows = jnp.einsum("bhqk,bhkd->bhqd", attention.astype(jnp.float32), value_rows)
    return rows_first(merged_rows, row_total)


def owner_transfer(
    landed_rows,
    landed_cotangent,
    row_presence,
    block_listing,
    scale_factors,
    input_weight,
    output_weight,
):
    normed, norm_pull = jax.vjp(
        lambda input_operand: layer_norm(input_operand, scale_factors), landed_rows
    )
    normed_half = normed.astype(jnp.bfloat16)
    packed_rows = jnp.dot(normed_half, input_weight, preferred_element_type=jnp.float32).astype(
        jnp.bfloat16
    )
    merged_rows, central_gather = jax.vjp(
        lambda input_operand: cross_account_inner(input_operand, row_presence, block_listing),
        packed_rows,
    )
    result = jnp.dot(merged_rows, output_weight, preferred_element_type=jnp.float32).astype(
        jnp.bfloat16
    )
    back_mixed = lax.dot_general(
        landed_cotangent,
        output_weight,
        (((1,), (1,)), ((), ())),
        preferred_element_type=jnp.float32,
    ).astype(jnp.bfloat16)
    back_packed = central_gather(back_mixed)[0]
    back_normed = lax.dot_general(
        back_packed, input_weight, (((1,), (1,)), ((), ())), preferred_element_type=jnp.float32
    )
    back_rows = norm_pull(back_normed)[0]
    return (result, back_rows, normed_half, back_packed, merged_rows)


def contract(left_part, right_part):
    return lax.dot_general(
        left_part, right_part, (((0,), (0,)), ((), ())), preferred_element_type=jnp.float32
    )


def sum_leading(stacked):
    total = stacked[0].astype(jnp.float32)
    for index in range(1, stacked.shape[0]):
        total = total + stacked[index].astype(jnp.float32)
    return total


def replica_sums(partial, replicas, owners):
    rows, width = partial.shape
    per_device = rows // owners // replicas
    terms = partial.astype(jnp.bfloat16).reshape(owners, replicas, per_device, width)
    terms = jnp.swapaxes(terms, 0, 1)
    terms = lax.all_to_all(terms, "dp", 0, 0, tiled=True)
    return sum_leading(terms).astype(jnp.bfloat16)


def gather_replicas(piece, replicas):
    copies = jnp.broadcast_to(piece[None], (replicas,) + piece.shape)
    gathered = lax.all_to_all(copies, "dp", 0, 0, tiled=True)
    return gathered.reshape(-1, piece.shape[-1])


def on_device(
    events,
    cotangent,
    intra_gain,
    intra_proj,
    intra_out,
    cross_norm_gain,
    cross_input_weight,
    cross_output_weight,
    owner_map,
    block_lists,
):
    rows_here = events[0]
    upstream = cotangent[0]
    local_rows, features = rows_here.shape
    owners = lax.axis_size("ev")
    replicas = lax.axis_size("dp")
    own_index = lax.axis_index("ev")
    row_capacity = 2 * local_rows // owners
    buffer_rows = owners * row_capacity
    hidden, intra_pull = jax.vjp(
        lambda input_operand: intra_branch(input_operand, intra_gain, intra_proj, intra_out),
        rows_here,
    )
    targets = owner_map[0]
    onehot = (targets[:, None] == jnp.arange(owners, dtype=jnp.int32)[None, :]).astype(jnp.int32)
    row_counts = jnp.sum(onehot.reshape(owners, local_rows, owners), axis=1)
    inbound_rows = lax.dynamic_index_in_dim(row_counts, own_index, axis=1, keepdims=False)
    own_onehot = lax.dynamic_slice_in_dim(onehot, own_index * local_rows, local_rows, 0)
    before = jnp.cumsum(own_onehot, axis=0) - own_onehot
    slot_ids = jnp.sum(before * own_onehot, axis=1)
    own_dest = lax.dynamic_slice_in_dim(targets, own_index * local_rows, local_rows, 0)
    position = own_dest * row_capacity + slot_ids
    placement = (
        jnp.arange(buffer_rows, dtype=jnp.int32)[:, None] == position[None, :]
    ).astype(jnp.bfloat16)
    both = jnp.concatenate([hidden, upstream], axis=1)
    outgoing = jnp.dot(placement, both, preferred_element_type=jnp.float32).astype(jnp.bfloat16)
    landed = lax.all_to_all(outgoing, "ev", split_axis=0, concat_axis=0, tiled=True)
    landed_rows = landed[:, :features]
    landed_cotangent = landed[:, features:]
    row_presence = (
        jnp.arange(row_capacity, dtype=jnp.int32)[None, :] < inbound_rows[:, None]
    ).reshape(buffer_rows)
    block_listing = block_lists[0, 0]
    result, back_rows, normed_half, back_packed, merged_rows = owner_transfer(
        landed_rows,
        landed_cotangent,
        row_presence,
        block_listing,
        cross_norm_gain,
        cross_input_weight,
        cross_output_weight,
    )
    factor = (replicas * owners * local_rows) ** (-0.5)
    partial_sum = jnp.concatenate(
        [contract(normed_half, back_packed), contract(merged_rows, landed_cotangent)], axis=1
    )
    weight_terms = replica_sums(partial_sum, replicas, owners)
    going_back = jnp.concatenate([result, back_rows.astype(jnp.bfloat16)], axis=1)
    payload = jnp.concatenate(
        [going_back.reshape(owners, -1), weight_terms.reshape(owners, -1)], axis=1
    )
    arrived = lax.all_to_all(payload, "ev", split_axis=0, concat_axis=0, tiled=True)
    split_at = going_back.size // owners
    came_back = arrived[:, :split_at].reshape(going_back.shape)
    owner_terms = arrived[:, split_at:].reshape((owners,) + weight_terms.shape[1:])
    portion = gather_replicas(sum_leading(owner_terms), replicas) * factor
    picked = lax.dot_general(
        placement, came_back, (((0,), (0,)), ((), ())), preferred_element_type=jnp.float32
    )
    layer_out = (hidden.astype(jnp.float32) + picked[:, :features]).astype(jnp.bfloat16)
    grad_hidden = (upstream.astype(jnp.float32) + picked[:, features:]).astype(jnp.bfloat16)
    grad_rows = intra_pull(grad_hidden)[0]
    return (
        layer_out[None],
        grad_rows[None],
        portion[:, : 3 * features],
        portion[:, 3 * features :],
    )


def solution(mesh):
    return jax.shard_map(
        on_device,
        mesh=mesh,
        in_specs=(
            P("dp", "ev", None),
            P("dp", "ev", None),
            P(),
            P(),
            P(),
            P(),
            P(),
            P(),
            P("dp", None),
            P("dp", "ev", None, None),
        ),
        out_specs=(P("dp", "ev", None), P("dp", "ev", None), P("ev", None), P("ev", None)),
        check_vma=False,
    )
```

```python
import jax
import jax.numpy as jnp
from jax import lax
from jax.sharding import PartitionSpec as P

HEADS = 8
HEAD_DIM = 64
EVENTS_PER_BLOCK = 128


EPSILON = 1e-05


def layer_norm(values, scale_factors):
    upcast = values.astype(jnp.float32)
    center = upcast - jnp.mean(upcast, axis=-1, keepdims=True)
    spread = jnp.mean(center * center, axis=-1, keepdims=True)
    return center * lax.rsqrt(spread + EPSILON) * scale_factors


def split_heads(matrix, block_groups):
    return matrix.reshape(block_groups, EVENTS_PER_BLOCK, HEADS, HEAD_DIM)


def heads_first(packed_rows, block_groups):
    parts = packed_rows.reshape(block_groups, EVENTS_PER_BLOCK, 3, HEADS, HEAD_DIM)
    return jnp.transpose(parts, (2, 0, 3, 1, 4)).astype(jnp.float32)


def rows_first(merged, row_total):
    return jnp.transpose(merged, (0, 2, 1, 3)).astype(jnp.bfloat16).reshape(row_total, -1)


def intra_branch(source, scale_factors, input_weight, output_weight):
    row_total, features = source.shape
    block_groups = row_total // EVENTS_PER_BLOCK
    normed = layer_norm(source, scale_factors).astype(jnp.bfloat16)
    packed_rows = jnp.dot(normed, input_weight, preferred_element_type=jnp.float32).astype(
        jnp.bfloat16
    )
    parts = heads_first(packed_rows, block_groups)
    queries, key_rows, value_rows = parts[0], parts[1], parts[2]
    scores = jnp.einsum("bhqd,bhkd->bhqk", queries, key_rows) * HEAD_DIM ** (-0.5)
    highest = jnp.max(scores, axis=-1, keepdims=True)
    weights = jnp.exp(scores - highest)
    attention = (weights / jnp.sum(weights, axis=-1, keepdims=True)).astype(jnp.bfloat16)
    merged_rows = jnp.einsum("bhqk,bhkd->bhqd", attention.astype(jnp.float32), value_rows)
    merged_rows = rows_first(merged_rows, row_total)
    branch = jnp.dot(merged_rows, output_weight, preferred_element_type=jnp.float32)
    return (source.astype(jnp.float32) + branch).astype(jnp.bfloat16)


def pick_block(blocks, chosen):
    picked = blocks[0]
    for index in range(1, blocks.shape[0]):
        picked = jnp.where(chosen == index, blocks[index], picked)
    return picked


def gather_segments(blocks, selected_rows, axis):
    block_groups, segments = selected_rows.shape
    return jnp.stack(
        [
            jnp.concatenate(
                [pick_block(blocks, selected_rows[group, segment]) for segment in range(segments)],
                axis=axis,
            )
            for group in range(block_groups)
        ],
        axis=0,
    )


def cross_account_inner(packed_rows, row_presence, block_listing):
    row_total, three_wide = packed_rows.shape
    block_groups = row_total // EVENTS_PER_BLOCK
    selected_rows = jnp.concatenate(
        [jnp.arange(block_groups, dtype=jnp.int32)[:, None], block_listing], axis=1
    )
    parts = heads_first(packed_rows, block_groups)
    queries = parts[0]
    key_rows = gather_segments(parts[1], selected_rows, 1)
    value_rows = gather_segments(parts[2], selected_rows, 1)
    presence_blocks = row_presence.reshape(block_groups, EVENTS_PER_BLOCK)
    key_present = gather_segments(presence_blocks, selected_rows, 0)
    key_total = key_present.shape[1]
    itself = (
        jnp.arange(key_total, dtype=jnp.int32)[None, :]
        == jnp.arange(EVENTS_PER_BLOCK, dtype=jnp.int32)[:, None]
    )
    allowed = key_present[:, None, None, :] | itself[None, None, :, :]
    scores = jnp.einsum("bhqd,bhkd->bhqk", queries, key_rows) * HEAD_DIM ** (-0.5)
    scores = jnp.where(allowed, scores, -1e30)
    highest = jnp.max(scores, axis=-1, keepdims=True)
    weights = jnp.where(allowed, jnp.exp(scores - highest), 0.0)
    attention = (weights / jnp.sum(weights, axis=-1, keepdims=True)).astype(jnp.bfloat16)
    merged_rows = jnp.einsum("bhqk,bhkd->bhqd", attention.astype(jnp.float32), value_rows)
    return rows_first(merged_rows, row_total)


def owner_transfer(
    landed_rows,
    landed_cotangent,
    row_presence,
    block_listing,
    scale_factors,
    input_weight,
    output_weight,
):
    normed, norm_pull = jax.vjp(
        lambda input_operand: layer_norm(input_operand, scale_factors), landed_rows
    )
    normed_half = normed.astype(jnp.bfloat16)
    packed_rows = jnp.dot(normed_half, input_weight, preferred_element_type=jnp.float32).astype(
        jnp.bfloat16
    )
    merged_rows, central_gather = jax.vjp(
        lambda input_operand: cross_account_inner(input_operand, row_presence, block_listing),
        packed_rows,
    )
    result = jnp.dot(merged_rows, output_weight, preferred_element_type=jnp.float32).astype(
        jnp.bfloat16
    )
    back_mixed = lax.dot_general(
        landed_cotangent,
        output_weight,
        (((1,), (1,)), ((), ())),
        preferred_element_type=jnp.float32,
    ).astype(jnp.bfloat16)
    back_packed = central_gather(back_mixed)[0]
    back_normed = lax.dot_general(
        back_packed, input_weight, (((1,), (1,)), ((), ())), preferred_element_type=jnp.float32
    )
    back_rows = norm_pull(back_normed)[0]
    return (result, back_rows, normed_half, back_packed, merged_rows)


def contract(left_part, right_part):
    return lax.dot_general(
        left_part, right_part, (((0,), (0,)), ((), ())), preferred_element_type=jnp.float32
    )


def feature_order(left_part, replicas, owners):
    rows, features = left_part.shape
    per_device = features // owners // replicas
    split = left_part.reshape(rows, owners, replicas, per_device)
    return jnp.swapaxes(split, 1, 2).reshape(rows, features)


def reduce_weight_terms(partial, replicas, owners):
    rows, width = partial.shape
    per_replica = rows // replicas
    per_device = per_replica // owners
    terms = partial.astype(jnp.bfloat16).reshape(replicas, per_replica, width)
    terms = lax.all_to_all(terms, "dp", 0, 0, tiled=True)
    terms = jnp.sum(terms.astype(jnp.float32), axis=0).astype(jnp.bfloat16)
    terms = terms.reshape(owners, per_device, width)
    terms = lax.all_to_all(terms, "ev", 0, 0, tiled=True)
    piece = jnp.sum(terms.astype(jnp.float32), axis=0)
    copies = jnp.broadcast_to(piece[None], (replicas, per_device, width))
    gathered = lax.all_to_all(copies, "dp", 0, 0, tiled=True)
    return gathered.reshape(replicas * per_device, width)


def on_device(
    events,
    cotangent,
    intra_gain,
    intra_proj,
    intra_out,
    cross_norm_gain,
    cross_input_weight,
    cross_output_weight,
    owner_map,
    block_lists,
):
    rows_here = events[0]
    upstream = cotangent[0]
    local_rows, features = rows_here.shape
    owners = lax.axis_size("ev")
    replicas = lax.axis_size("dp")
    own_index = lax.axis_index("ev")
    row_capacity = 2 * local_rows // owners
    buffer_rows = owners * row_capacity
    hidden, intra_pull = jax.vjp(
        lambda input_operand: intra_branch(input_operand, intra_gain, intra_proj, intra_out),
        rows_here,
    )
    targets = owner_map[0]
    onehot = (targets[:, None] == jnp.arange(owners, dtype=jnp.int32)[None, :]).astype(jnp.int32)
    row_counts = jnp.sum(onehot.reshape(owners, local_rows, owners), axis=1)
    inbound_rows = lax.dynamic_index_in_dim(row_counts, own_index, axis=1, keepdims=False)
    own_onehot = lax.dynamic_slice_in_dim(onehot, own_index * local_rows, local_rows, 0)
    before = jnp.cumsum(own_onehot, axis=0) - own_onehot
    slot_ids = jnp.sum(before * own_onehot, axis=1)
    own_dest = lax.dynamic_slice_in_dim(targets, own_index * local_rows, local_rows, 0)
    position = own_dest * row_capacity + slot_ids
    placement = (
        jnp.arange(buffer_rows, dtype=jnp.int32)[:, None] == position[None, :]
    ).astype(jnp.bfloat16)
    both = jnp.concatenate([hidden, upstream], axis=1)
    outgoing = jnp.dot(placement, both, preferred_element_type=jnp.float32).astype(jnp.bfloat16)
    landed = lax.all_to_all(outgoing, "ev", split_axis=0, concat_axis=0, tiled=True)
    landed_rows = landed[:, :features]
    landed_cotangent = landed[:, features:]
    row_presence = (
        jnp.arange(row_capacity, dtype=jnp.int32)[None, :] < inbound_rows[:, None]
    ).reshape(buffer_rows)
    block_listing = block_lists[0, 0]
    result, back_rows, normed_half, back_packed, merged_rows = owner_transfer(
        landed_rows,
        landed_cotangent,
        row_presence,
        block_listing,
        cross_norm_gain,
        cross_input_weight,
        cross_output_weight,
    )
    going_back = jnp.concatenate([result, back_rows.astype(jnp.bfloat16)], axis=1)
    came_back = lax.all_to_all(going_back, "ev", split_axis=0, concat_axis=0, tiled=True)
    picked = lax.dot_general(
        placement, came_back, (((0,), (0,)), ((), ())), preferred_element_type=jnp.float32
    )
    layer_out = (hidden.astype(jnp.float32) + picked[:, :features]).astype(jnp.bfloat16)
    grad_hidden = (upstream.astype(jnp.float32) + picked[:, features:]).astype(jnp.bfloat16)
    grad_rows = intra_pull(grad_hidden)[0]
    factor = (replicas * owners * local_rows) ** (-0.5)
    partial_sum = jnp.concatenate(
        [
            contract(feature_order(normed_half, replicas, owners), back_packed),
            contract(feature_order(merged_rows, replicas, owners), landed_cotangent),
        ],
        axis=1,
    )
    portion = reduce_weight_terms(partial_sum, replicas, owners) * factor
    return (
        layer_out[None],
        grad_rows[None],
        portion[:, : 3 * features],
        portion[:, 3 * features :],
    )


def solution(mesh):
    return jax.shard_map(
        on_device,
        mesh=mesh,
        in_specs=(
            P("dp", "ev", None),
            P("dp", "ev", None),
            P(),
            P(),
            P(),
            P(),
            P(),
            P(),
            P("dp", None),
            P("dp", "ev", None, None),
        ),
        out_specs=(P("dp", "ev", None), P("dp", "ev", None), P("ev", None), P("ev", None)),
        check_vma=False,
    )
```

```python
import jax
import jax.numpy as jnp
from jax import lax
from jax.sharding import PartitionSpec as P

HEADS = 8
HEAD_DIM = 64
EVENTS_PER_BLOCK = 128


EPSILON = 1e-05


def layer_norm(values, scale_factors):
    upcast = values.astype(jnp.float32)
    center = upcast - jnp.mean(upcast, axis=-1, keepdims=True)
    spread = jnp.mean(center * center, axis=-1, keepdims=True)
    return center * lax.rsqrt(spread + EPSILON) * scale_factors


def split_heads(matrix, block_groups):
    return matrix.reshape(block_groups, EVENTS_PER_BLOCK, HEADS, HEAD_DIM)


def project_heads(normed, input_weight):
    row_total, features = normed.shape
    block_groups = row_total // EVENTS_PER_BLOCK
    weight = input_weight.reshape(features, 3, HEADS, HEAD_DIM)
    blocks = normed.reshape(block_groups, EVENTS_PER_BLOCK, features)
    return jnp.einsum(
        "bqf,fphd->pbhqd", blocks, weight, preferred_element_type=jnp.float32
    ).astype(jnp.bfloat16)


def rows_first(merged, row_total):
    return jnp.transpose(merged, (0, 2, 1, 3)).astype(jnp.bfloat16).reshape(row_total, -1)


def intra_branch(source, scale_factors, input_weight, output_weight):
    row_total, features = source.shape
    block_groups = row_total // EVENTS_PER_BLOCK
    normed = layer_norm(source, scale_factors).astype(jnp.bfloat16)
    parts = project_heads(normed, input_weight).astype(jnp.float32)
    queries, key_rows, value_rows = parts[0], parts[1], parts[2]
    scores = jnp.einsum("bhqd,bhkd->bhqk", queries, key_rows) * HEAD_DIM ** (-0.5)
    highest = jnp.max(scores, axis=-1, keepdims=True)
    weights = jnp.exp(scores - highest)
    attention = (weights / jnp.sum(weights, axis=-1, keepdims=True)).astype(jnp.bfloat16)
    merged_rows = jnp.einsum("bhqk,bhkd->bhqd", attention.astype(jnp.float32), value_rows)
    merged_rows = rows_first(merged_rows, row_total)
    branch = jnp.dot(merged_rows, output_weight, preferred_element_type=jnp.float32)
    return (source.astype(jnp.float32) + branch).astype(jnp.bfloat16)


def pick_block(blocks, chosen):
    picked = blocks[0]
    for index in range(1, blocks.shape[0]):
        picked = jnp.where(chosen == index, blocks[index], picked)
    return picked


def gather_segments(blocks, selected_rows, axis):
    block_groups, segments = selected_rows.shape
    return jnp.stack(
        [
            jnp.concatenate(
                [pick_block(blocks, selected_rows[group, segment]) for segment in range(segments)],
                axis=axis,
            )
            for group in range(block_groups)
        ],
        axis=0,
    )


def cross_account_inner(packed_heads, row_presence, block_listing):
    block_groups = packed_heads.shape[1]
    row_total = block_groups * EVENTS_PER_BLOCK
    selected_rows = jnp.concatenate(
        [jnp.arange(block_groups, dtype=jnp.int32)[:, None], block_listing], axis=1
    )
    parts = packed_heads.astype(jnp.float32)
    queries = parts[0]
    key_rows = gather_segments(parts[1], selected_rows, 1)
    value_rows = gather_segments(parts[2], selected_rows, 1)
    presence_blocks = row_presence.reshape(block_groups, EVENTS_PER_BLOCK)
    key_present = gather_segments(presence_blocks, selected_rows, 0)
    key_total = key_present.shape[1]
    itself = (
        jnp.arange(key_total, dtype=jnp.int32)[None, :]
        == jnp.arange(EVENTS_PER_BLOCK, dtype=jnp.int32)[:, None]
    )
    allowed = key_present[:, None, None, :] | itself[None, None, :, :]
    scores = jnp.einsum("bhqd,bhkd->bhqk", queries, key_rows) * HEAD_DIM ** (-0.5)
    scores = jnp.where(allowed, scores, -1e30)
    highest = jnp.max(scores, axis=-1, keepdims=True)
    weights = jnp.where(allowed, jnp.exp(scores - highest), 0.0)
    attention = (weights / jnp.sum(weights, axis=-1, keepdims=True)).astype(jnp.bfloat16)
    merged_rows = jnp.einsum("bhqk,bhkd->bhqd", attention.astype(jnp.float32), value_rows)
    return rows_first(merged_rows, row_total)


def owner_transfer(
    landed_rows,
    landed_cotangent,
    row_presence,
    block_listing,
    scale_factors,
    input_weight,
    output_weight,
):
    normed, norm_pull = jax.vjp(
        lambda input_operand: layer_norm(input_operand, scale_factors), landed_rows
    )
    normed_half = normed.astype(jnp.bfloat16)
    packed_heads = project_heads(normed_half, input_weight)
    merged_rows, central_gather = jax.vjp(
        lambda input_operand: cross_account_inner(input_operand, row_presence, block_listing),
        packed_heads,
    )
    result = jnp.dot(merged_rows, output_weight, preferred_element_type=jnp.float32).astype(
        jnp.bfloat16
    )
    back_mixed = lax.dot_general(
        landed_cotangent,
        output_weight,
        (((1,), (1,)), ((), ())),
        preferred_element_type=jnp.float32,
    ).astype(jnp.bfloat16)
    back_packed = central_gather(back_mixed)[0]
    features = normed_half.shape[1]
    back_normed = jnp.einsum(
        "pbhqd,fphd->bqf",
        back_packed,
        input_weight.reshape(features, 3, HEADS, HEAD_DIM),
        preferred_element_type=jnp.float32,
    ).reshape(normed_half.shape)
    back_rows = norm_pull(back_normed)[0]
    return (result, back_rows, normed_half, back_packed, merged_rows)


def contract(left_part, right_part):
    return lax.dot_general(
        left_part, right_part, (((0,), (0,)), ((), ())), preferred_element_type=jnp.float32
    )


def feature_order(left_part, replicas, owners):
    rows, features = left_part.shape
    per_device = features // owners // replicas
    split = left_part.reshape(rows, owners, replicas, per_device)
    return jnp.swapaxes(split, 1, 2).reshape(rows, features)


def reduce_weight_terms(partial, replicas, owners):
    rows, width = partial.shape
    per_replica = rows // replicas
    per_device = per_replica // owners
    terms = partial.astype(jnp.bfloat16).reshape(replicas, per_replica, width)
    terms = lax.all_to_all(terms, "dp", 0, 0, tiled=True)
    terms = jnp.sum(terms.astype(jnp.float32), axis=0).astype(jnp.bfloat16)
    terms = terms.reshape(owners, per_device, width)
    terms = lax.all_to_all(terms, "ev", 0, 0, tiled=True)
    piece = jnp.sum(terms.astype(jnp.float32), axis=0)
    copies = jnp.broadcast_to(piece[None], (replicas, per_device, width))
    gathered = lax.all_to_all(copies, "dp", 0, 0, tiled=True)
    return gathered.reshape(replicas * per_device, width)


def on_device(
    events,
    cotangent,
    intra_gain,
    intra_proj,
    intra_out,
    cross_norm_gain,
    cross_input_weight,
    cross_output_weight,
    owner_map,
    block_lists,
):
    rows_here = events[0]
    upstream = cotangent[0]
    local_rows, features = rows_here.shape
    owners = lax.axis_size("ev")
    replicas = lax.axis_size("dp")
    own_index = lax.axis_index("ev")
    row_capacity = 2 * local_rows // owners
    buffer_rows = owners * row_capacity
    hidden, intra_pull = jax.vjp(
        lambda input_operand: intra_branch(input_operand, intra_gain, intra_proj, intra_out),
        rows_here,
    )
    targets = owner_map[0]
    onehot = (targets[:, None] == jnp.arange(owners, dtype=jnp.int32)[None, :]).astype(jnp.int32)
    row_counts = jnp.sum(onehot.reshape(owners, local_rows, owners), axis=1)
    inbound_rows = lax.dynamic_index_in_dim(row_counts, own_index, axis=1, keepdims=False)
    own_onehot = lax.dynamic_slice_in_dim(onehot, own_index * local_rows, local_rows, 0)
    before = jnp.cumsum(own_onehot, axis=0) - own_onehot
    slot_ids = jnp.sum(before * own_onehot, axis=1)
    own_dest = lax.dynamic_slice_in_dim(targets, own_index * local_rows, local_rows, 0)
    position = own_dest * row_capacity + slot_ids
    placement = (
        jnp.arange(buffer_rows, dtype=jnp.int32)[:, None] == position[None, :]
    ).astype(jnp.bfloat16)
    both = jnp.concatenate([hidden, upstream], axis=1)
    outgoing = jnp.dot(placement, both, preferred_element_type=jnp.float32).astype(jnp.bfloat16)
    landed = lax.all_to_all(outgoing, "ev", split_axis=0, concat_axis=0, tiled=True)
    landed_rows = landed[:, :features]
    landed_cotangent = landed[:, features:]
    row_presence = (
        jnp.arange(row_capacity, dtype=jnp.int32)[None, :] < inbound_rows[:, None]
    ).reshape(buffer_rows)
    block_listing = block_lists[0, 0]
    result, back_rows, normed_half, back_packed, merged_rows = owner_transfer(
        landed_rows,
        landed_cotangent,
        row_presence,
        block_listing,
        cross_norm_gain,
        cross_input_weight,
        cross_output_weight,
    )
    going_back = jnp.concatenate([result, back_rows.astype(jnp.bfloat16)], axis=1)
    came_back = lax.all_to_all(going_back, "ev", split_axis=0, concat_axis=0, tiled=True)
    picked = lax.dot_general(
        placement, came_back, (((0,), (0,)), ((), ())), preferred_element_type=jnp.float32
    )
    layer_out = (hidden.astype(jnp.float32) + picked[:, :features]).astype(jnp.bfloat16)
    grad_hidden = (upstream.astype(jnp.float32) + picked[:, features:]).astype(jnp.bfloat16)
    grad_rows = intra_pull(grad_hidden)[0]
    factor = (replicas * owners * local_rows) ** (-0.5)
    partial_sum = jnp.concatenate(
        [
            jnp.einsum(
                "bqf,pbhqd->fphd",
                feature_order(normed_half, replicas, owners).reshape(back_packed.shape[1], -1, features),
                back_packed,
                preferred_element_type=jnp.float32,
            ).reshape(features, -1),
            contract(feature_order(merged_rows, replicas, owners), landed_cotangent),
        ],
        axis=1,
    )
    portion = reduce_weight_terms(partial_sum, replicas, owners) * factor
    return (
        layer_out[None],
        grad_rows[None],
        portion[:, : 3 * features],
        portion[:, 3 * features :],
    )


def solution(mesh):
    return jax.shard_map(
        on_device,
        mesh=mesh,
        in_specs=(
            P("dp", "ev", None),
            P("dp", "ev", None),
            P(),
            P(),
            P(),
            P(),
            P(),
            P(),
            P("dp", None),
            P("dp", "ev", None, None),
        ),
        out_specs=(P("dp", "ev", None), P("dp", "ev", None), P("ev", None), P("ev", None)),
        check_vma=False,
    )
```

```python
import jax
import jax.numpy as jnp
from jax import lax
from jax.sharding import PartitionSpec as P

HEADS = 8
HEAD_DIM = 64
EVENTS_PER_BLOCK = 128


EPSILON = 1e-05


def layer_norm(values, scale_factors):
    upcast = values.astype(jnp.float32)
    center = upcast - jnp.mean(upcast, axis=-1, keepdims=True)
    spread = jnp.mean(center * center, axis=-1, keepdims=True)
    return center * lax.rsqrt(spread + EPSILON) * scale_factors


def split_heads(matrix, block_groups):
    return matrix.reshape(block_groups, EVENTS_PER_BLOCK, HEADS, HEAD_DIM)


def heads_first(packed_rows, block_groups):
    parts = packed_rows.reshape(block_groups, EVENTS_PER_BLOCK, 3, HEADS, HEAD_DIM)
    return jnp.transpose(parts, (2, 0, 3, 1, 4)).astype(jnp.float32)


def rows_first(merged, row_total):
    return jnp.transpose(merged, (0, 2, 1, 3)).astype(jnp.bfloat16).reshape(row_total, -1)


def intra_branch(source, scale_factors, input_weight, output_weight):
    row_total, features = source.shape
    block_groups = row_total // EVENTS_PER_BLOCK
    normed = layer_norm(source, scale_factors).astype(jnp.bfloat16)
    packed_rows = jnp.dot(normed, input_weight, preferred_element_type=jnp.float32).astype(
        jnp.bfloat16
    )
    parts = heads_first(packed_rows, block_groups)
    queries, key_rows, value_rows = parts[0], parts[1], parts[2]
    scores = jnp.einsum("bhqd,bhkd->bhqk", queries, key_rows) * HEAD_DIM ** (-0.5)
    highest = jnp.max(scores, axis=-1, keepdims=True)
    weights = jnp.exp(scores - highest)
    attention = (weights / jnp.sum(weights, axis=-1, keepdims=True)).astype(jnp.bfloat16)
    merged_rows = jnp.einsum("bhqk,bhkd->bhqd", attention.astype(jnp.float32), value_rows)
    merged_rows = rows_first(merged_rows, row_total)
    branch = jnp.dot(merged_rows, output_weight, preferred_element_type=jnp.float32)
    return (source.astype(jnp.float32) + branch).astype(jnp.bfloat16)


def pick_block(blocks, chosen):
    picked = blocks[0]
    for index in range(1, blocks.shape[0]):
        picked = jnp.where(chosen == index, blocks[index], picked)
    return picked


def gather_segments(blocks, selected_rows, axis):
    block_groups, segments = selected_rows.shape
    return jnp.stack(
        [
            jnp.concatenate(
                [pick_block(blocks, selected_rows[group, segment]) for segment in range(segments)],
                axis=axis,
            )
            for group in range(block_groups)
        ],
        axis=0,
    )


def head_mask(features):
    lanes = jnp.arange(features, dtype=jnp.int32) // HEAD_DIM
    return (lanes[None, :] == jnp.arange(HEADS, dtype=jnp.int32)[:, None]).astype(jnp.float32)


def cross_account_inner(packed_rows, row_presence, block_listing):
    row_total, three_wide = packed_rows.shape
    features = three_wide // 3
    block_groups = row_total // EVENTS_PER_BLOCK
    selected_rows = jnp.concatenate(
        [jnp.arange(block_groups, dtype=jnp.int32)[:, None], block_listing], axis=1
    )
    by_block = packed_rows.astype(jnp.float32).reshape(block_groups, EVENTS_PER_BLOCK, three_wide)
    queries = by_block[:, :, :features]
    key_rows = gather_segments(by_block[:, :, features : 2 * features], selected_rows, 0)
    value_rows = gather_segments(by_block[:, :, 2 * features :], selected_rows, 0)
    presence_blocks = row_presence.reshape(block_groups, EVENTS_PER_BLOCK)
    key_present = gather_segments(presence_blocks, selected_rows, 0)
    key_total = key_present.shape[1]
    itself = (
        jnp.arange(key_total, dtype=jnp.int32)[None, :]
        == jnp.arange(EVENTS_PER_BLOCK, dtype=jnp.int32)[:, None]
    )
    allowed = key_present[:, None, None, :] | itself[None, None, :, :]
    mask = head_mask(features)
    masked_queries = queries[:, None, :, :] * mask[None, :, None, :]
    scores = jnp.einsum("bhqf,bkf->bhqk", masked_queries, key_rows) * HEAD_DIM ** (-0.5)
    scores = jnp.where(allowed, scores, -1e30)
    highest = jnp.max(scores, axis=-1, keepdims=True)
    weights = jnp.where(allowed, jnp.exp(scores - highest), 0.0)
    attention = (weights / jnp.sum(weights, axis=-1, keepdims=True)).astype(jnp.bfloat16)
    per_head = jnp.einsum("bhqk,bkf->bhqf", attention.astype(jnp.float32), value_rows)
    merged_rows = jnp.sum(per_head * mask[None, :, None, :], axis=1)
    return merged_rows.astype(jnp.bfloat16).reshape(row_total, features)


def owner_transfer(
    landed_rows,
    landed_cotangent,
    row_presence,
    block_listing,
    scale_factors,
    input_weight,
    output_weight,
):
    normed, norm_pull = jax.vjp(
        lambda input_operand: layer_norm(input_operand, scale_factors), landed_rows
    )
    normed_half = normed.astype(jnp.bfloat16)
    packed_rows = jnp.dot(normed_half, input_weight, preferred_element_type=jnp.float32).astype(
        jnp.bfloat16
    )
    merged_rows, central_gather = jax.vjp(
        lambda input_operand: cross_account_inner(input_operand, row_presence, block_listing),
        packed_rows,
    )
    result = jnp.dot(merged_rows, output_weight, preferred_element_type=jnp.float32).astype(
        jnp.bfloat16
    )
    back_mixed = lax.dot_general(
        landed_cotangent,
        output_weight,
        (((1,), (1,)), ((), ())),
        preferred_element_type=jnp.float32,
    ).astype(jnp.bfloat16)
    back_packed = central_gather(back_mixed)[0]
    back_normed = lax.dot_general(
        back_packed, input_weight, (((1,), (1,)), ((), ())), preferred_element_type=jnp.float32
    )
    back_rows = norm_pull(back_normed)[0]
    return (result, back_rows, normed_half, back_packed, merged_rows)


def contract(left_part, right_part):
    return lax.dot_general(
        left_part, right_part, (((0,), (0,)), ((), ())), preferred_element_type=jnp.float32
    )


def feature_order(left_part, replicas, owners):
    rows, features = left_part.shape
    per_device = features // owners // replicas
    split = left_part.reshape(rows, owners, replicas, per_device)
    return jnp.swapaxes(split, 1, 2).reshape(rows, features)


def reduce_weight_terms(partial, replicas, owners):
    rows, width = partial.shape
    per_replica = rows // replicas
    per_device = per_replica // owners
    terms = partial.astype(jnp.bfloat16).reshape(replicas, per_replica, width)
    terms = lax.all_to_all(terms, "dp", 0, 0, tiled=True)
    terms = jnp.sum(terms.astype(jnp.float32), axis=0).astype(jnp.bfloat16)
    terms = terms.reshape(owners, per_device, width)
    terms = lax.all_to_all(terms, "ev", 0, 0, tiled=True)
    piece = jnp.sum(terms.astype(jnp.float32), axis=0)
    copies = jnp.broadcast_to(piece[None], (replicas, per_device, width))
    gathered = lax.all_to_all(copies, "dp", 0, 0, tiled=True)
    return gathered.reshape(replicas * per_device, width)


def on_device(
    events,
    cotangent,
    intra_gain,
    intra_proj,
    intra_out,
    cross_norm_gain,
    cross_input_weight,
    cross_output_weight,
    owner_map,
    block_lists,
):
    rows_here = events[0]
    upstream = cotangent[0]
    local_rows, features = rows_here.shape
    owners = lax.axis_size("ev")
    replicas = lax.axis_size("dp")
    own_index = lax.axis_index("ev")
    row_capacity = 2 * local_rows // owners
    buffer_rows = owners * row_capacity
    hidden, intra_pull = jax.vjp(
        lambda input_operand: intra_branch(input_operand, intra_gain, intra_proj, intra_out),
        rows_here,
    )
    targets = owner_map[0]
    onehot = (targets[:, None] == jnp.arange(owners, dtype=jnp.int32)[None, :]).astype(jnp.int32)
    row_counts = jnp.sum(onehot.reshape(owners, local_rows, owners), axis=1)
    inbound_rows = lax.dynamic_index_in_dim(row_counts, own_index, axis=1, keepdims=False)
    own_onehot = lax.dynamic_slice_in_dim(onehot, own_index * local_rows, local_rows, 0)
    before = jnp.cumsum(own_onehot, axis=0) - own_onehot
    slot_ids = jnp.sum(before * own_onehot, axis=1)
    own_dest = lax.dynamic_slice_in_dim(targets, own_index * local_rows, local_rows, 0)
    position = own_dest * row_capacity + slot_ids
    placement = (
        jnp.arange(buffer_rows, dtype=jnp.int32)[:, None] == position[None, :]
    ).astype(jnp.bfloat16)
    both = jnp.concatenate([hidden, upstream], axis=1)
    outgoing = jnp.dot(placement, both, preferred_element_type=jnp.float32).astype(jnp.bfloat16)
    landed = lax.all_to_all(outgoing, "ev", split_axis=0, concat_axis=0, tiled=True)
    landed_rows = landed[:, :features]
    landed_cotangent = landed[:, features:]
    row_presence = (
        jnp.arange(row_capacity, dtype=jnp.int32)[None, :] < inbound_rows[:, None]
    ).reshape(buffer_rows)
    block_listing = block_lists[0, 0]
    result, back_rows, normed_half, back_packed, merged_rows = owner_transfer(
        landed_rows,
        landed_cotangent,
        row_presence,
        block_listing,
        cross_norm_gain,
        cross_input_weight,
        cross_output_weight,
    )
    going_back = jnp.concatenate([result, back_rows.astype(jnp.bfloat16)], axis=1)
    came_back = lax.all_to_all(going_back, "ev", split_axis=0, concat_axis=0, tiled=True)
    picked = lax.dot_general(
        placement, came_back, (((0,), (0,)), ((), ())), preferred_element_type=jnp.float32
    )
    layer_out = (hidden.astype(jnp.float32) + picked[:, :features]).astype(jnp.bfloat16)
    grad_hidden = (upstream.astype(jnp.float32) + picked[:, features:]).astype(jnp.bfloat16)
    grad_rows = intra_pull(grad_hidden)[0]
    factor = (replicas * owners * local_rows) ** (-0.5)
    partial_sum = jnp.concatenate(
        [
            contract(feature_order(normed_half, replicas, owners), back_packed),
            contract(feature_order(merged_rows, replicas, owners), landed_cotangent),
        ],
        axis=1,
    )
    portion = reduce_weight_terms(partial_sum, replicas, owners) * factor
    return (
        layer_out[None],
        grad_rows[None],
        portion[:, : 3 * features],
        portion[:, 3 * features :],
    )


def solution(mesh):
    return jax.shard_map(
        on_device,
        mesh=mesh,
        in_specs=(
            P("dp", "ev", None),
            P("dp", "ev", None),
            P(),
            P(),
            P(),
            P(),
            P(),
            P(),
            P("dp", None),
            P("dp", "ev", None, None),
        ),
        out_specs=(P("dp", "ev", None), P("dp", "ev", None), P("ev", None), P("ev", None)),
        check_vma=False,
    )
```

```python
import jax
import jax.numpy as jnp
from jax import lax
from jax.sharding import PartitionSpec as P

HEADS = 8
HEAD_DIM = 64
EVENTS_PER_BLOCK = 128


EPSILON = 1e-05


def layer_norm(values, scale_factors):
    upcast = values.astype(jnp.float32)
    center = upcast - jnp.mean(upcast, axis=-1, keepdims=True)
    spread = jnp.mean(center * center, axis=-1, keepdims=True)
    return center * lax.rsqrt(spread + EPSILON) * scale_factors


def split_heads(matrix, block_groups):
    return matrix.reshape(block_groups, EVENTS_PER_BLOCK, HEADS, HEAD_DIM)


def heads_first(packed_rows, block_groups):
    parts = packed_rows.reshape(block_groups, EVENTS_PER_BLOCK, 3, HEADS, HEAD_DIM)
    return jnp.transpose(parts, (2, 0, 3, 1, 4)).astype(jnp.float32)


def rows_first(merged, row_total):
    return jnp.transpose(merged, (0, 2, 1, 3)).astype(jnp.bfloat16).reshape(row_total, -1)


def intra_branch(source, scale_factors, input_weight, output_weight):
    row_total, features = source.shape
    block_groups = row_total // EVENTS_PER_BLOCK
    normed = layer_norm(source, scale_factors).astype(jnp.bfloat16)
    packed_rows = jnp.dot(normed, input_weight, preferred_element_type=jnp.float32).astype(
        jnp.bfloat16
    )
    parts = heads_first(packed_rows, block_groups)
    queries, key_rows, value_rows = parts[0], parts[1], parts[2]
    scores = jnp.einsum("bhqd,bhkd->bhqk", queries, key_rows) * HEAD_DIM ** (-0.5)
    highest = jnp.max(scores, axis=-1, keepdims=True)
    weights = jnp.exp(scores - highest)
    attention = (weights / jnp.sum(weights, axis=-1, keepdims=True)).astype(jnp.bfloat16)
    merged_rows = jnp.einsum("bhqk,bhkd->bhqd", attention.astype(jnp.float32), value_rows)
    merged_rows = rows_first(merged_rows, row_total)
    branch = jnp.dot(merged_rows, output_weight, preferred_element_type=jnp.float32)
    return (source.astype(jnp.float32) + branch).astype(jnp.bfloat16)


def pick_block(blocks, chosen):
    picked = blocks[0]
    for index in range(1, blocks.shape[0]):
        picked = jnp.where(chosen == index, blocks[index], picked)
    return picked


def gather_segments(blocks, selected_rows, axis):
    block_groups, segments = selected_rows.shape
    return jnp.stack(
        [
            jnp.concatenate(
                [pick_block(blocks, selected_rows[group, segment]) for segment in range(segments)],
                axis=axis,
            )
            for group in range(block_groups)
        ],
        axis=0,
    )


def head_mask(features):
    lanes = jnp.arange(features, dtype=jnp.int32) // HEAD_DIM
    return (lanes[None, :] == jnp.arange(HEADS, dtype=jnp.int32)[:, None]).astype(jnp.float32)


def cross_account_inner(packed_rows, row_presence, block_listing):
    row_total, three_wide = packed_rows.shape
    features = three_wide // 3
    block_groups = row_total // EVENTS_PER_BLOCK
    selected_rows = jnp.concatenate(
        [jnp.arange(block_groups, dtype=jnp.int32)[:, None], block_listing], axis=1
    )
    by_block = packed_rows.astype(jnp.float32).reshape(block_groups, EVENTS_PER_BLOCK, three_wide)
    queries = by_block[:, :, :features]
    key_rows = gather_segments(by_block[:, :, features : 2 * features], selected_rows, 0)
    value_rows = gather_segments(by_block[:, :, 2 * features :], selected_rows, 0)
    presence_blocks = row_presence.reshape(block_groups, EVENTS_PER_BLOCK)
    key_present = gather_segments(presence_blocks, selected_rows, 0)
    key_total = key_present.shape[1]
    itself = (
        jnp.arange(key_total, dtype=jnp.int32)[None, :]
        == jnp.arange(EVENTS_PER_BLOCK, dtype=jnp.int32)[:, None]
    )
    allowed = key_present[:, None, None, :] | itself[None, None, :, :]
    mask = head_mask(features)
    masked_queries = queries[:, None, :, :] * mask[None, :, None, :]
    scores = jnp.einsum("bhqf,bkf->bhqk", masked_queries, key_rows) * HEAD_DIM ** (-0.5)
    scores = jnp.where(allowed, scores, -1e30)
    highest = jnp.max(scores, axis=-1, keepdims=True)
    weights = jnp.where(allowed, jnp.exp(scores - highest), 0.0)
    attention = (weights / jnp.sum(weights, axis=-1, keepdims=True)).astype(jnp.bfloat16)
    per_head = jnp.einsum("bhqk,bkf->bhqf", attention.astype(jnp.float32), value_rows)
    merged_rows = jnp.sum(per_head * mask[None, :, None, :], axis=1)
    return merged_rows.astype(jnp.bfloat16).reshape(row_total, features)


def owner_transfer(
    landed_rows,
    landed_cotangent,
    row_presence,
    block_listing,
    scale_factors,
    input_weight,
    output_weight,
):
    normed, norm_pull = jax.vjp(
        lambda input_operand: layer_norm(input_operand, scale_factors), landed_rows
    )
    normed_half = normed.astype(jnp.bfloat16)
    packed_rows = jnp.dot(normed_half, input_weight, preferred_element_type=jnp.float32).astype(
        jnp.bfloat16
    )
    merged_rows, central_gather = jax.vjp(
        lambda input_operand: cross_account_inner(input_operand, row_presence, block_listing),
        packed_rows,
    )
    result = jnp.dot(merged_rows, output_weight, preferred_element_type=jnp.float32).astype(
        jnp.bfloat16
    )
    back_mixed = lax.dot_general(
        landed_cotangent,
        output_weight,
        (((1,), (1,)), ((), ())),
        preferred_element_type=jnp.float32,
    ).astype(jnp.bfloat16)
    back_packed = central_gather(back_mixed)[0]
    back_normed = lax.dot_general(
        back_packed, input_weight, (((1,), (1,)), ((), ())), preferred_element_type=jnp.float32
    )
    back_rows = norm_pull(back_normed)[0]
    return (result, back_rows, normed_half, back_packed, merged_rows)


def contract(left_part, right_part):
    return lax.dot_general(
        left_part, right_part, (((0,), (0,)), ((), ())), preferred_element_type=jnp.float32
    )


def ordered_contract(left_part, right_part, replicas, owners):
    rows, features = left_part.shape
    per_device = features // owners // replicas
    flipped = jnp.transpose(left_part).reshape(owners, replicas, per_device * rows)
    flipped = jnp.swapaxes(flipped, 0, 1).reshape(features, rows)
    return jnp.dot(flipped, right_part, preferred_element_type=jnp.float32)


def reduce_weight_terms(partial, replicas, owners):
    rows, width = partial.shape
    per_replica = rows // replicas
    per_device = per_replica // owners
    terms = partial.astype(jnp.bfloat16).reshape(replicas, per_replica, width)
    terms = lax.all_to_all(terms, "dp", 0, 0, tiled=True)
    terms = jnp.sum(terms.astype(jnp.float32), axis=0).astype(jnp.bfloat16)
    terms = terms.reshape(owners, per_device, width)
    terms = lax.all_to_all(terms, "ev", 0, 0, tiled=True)
    piece = jnp.sum(terms.astype(jnp.float32), axis=0)
    copies = jnp.broadcast_to(piece[None], (replicas, per_device, width))
    gathered = lax.all_to_all(copies, "dp", 0, 0, tiled=True)
    return gathered.reshape(replicas * per_device, width)


def on_device(
    events,
    cotangent,
    intra_gain,
    intra_proj,
    intra_out,
    cross_norm_gain,
    cross_input_weight,
    cross_output_weight,
    owner_map,
    block_lists,
):
    rows_here = events[0]
    upstream = cotangent[0]
    local_rows, features = rows_here.shape
    owners = lax.axis_size("ev")
    replicas = lax.axis_size("dp")
    own_index = lax.axis_index("ev")
    row_capacity = 2 * local_rows // owners
    buffer_rows = owners * row_capacity
    hidden, intra_pull = jax.vjp(
        lambda input_operand: intra_branch(input_operand, intra_gain, intra_proj, intra_out),
        rows_here,
    )
    targets = owner_map[0]
    onehot = (targets[:, None] == jnp.arange(owners, dtype=jnp.int32)[None, :]).astype(jnp.int32)
    row_counts = jnp.sum(onehot.reshape(owners, local_rows, owners), axis=1)
    inbound_rows = lax.dynamic_index_in_dim(row_counts, own_index, axis=1, keepdims=False)
    own_onehot = lax.dynamic_slice_in_dim(onehot, own_index * local_rows, local_rows, 0)
    before = jnp.cumsum(own_onehot, axis=0) - own_onehot
    slot_ids = jnp.sum(before * own_onehot, axis=1)
    own_dest = lax.dynamic_slice_in_dim(targets, own_index * local_rows, local_rows, 0)
    position = own_dest * row_capacity + slot_ids
    placement = (
        jnp.arange(buffer_rows, dtype=jnp.int32)[:, None] == position[None, :]
    ).astype(jnp.bfloat16)
    both = jnp.concatenate([hidden, upstream], axis=1)
    outgoing = jnp.dot(placement, both, preferred_element_type=jnp.float32).astype(jnp.bfloat16)
    landed = lax.all_to_all(outgoing, "ev", split_axis=0, concat_axis=0, tiled=True)
    landed_rows = landed[:, :features]
    landed_cotangent = landed[:, features:]
    row_presence = (
        jnp.arange(row_capacity, dtype=jnp.int32)[None, :] < inbound_rows[:, None]
    ).reshape(buffer_rows)
    block_listing = block_lists[0, 0]
    result, back_rows, normed_half, back_packed, merged_rows = owner_transfer(
        landed_rows,
        landed_cotangent,
        row_presence,
        block_listing,
        cross_norm_gain,
        cross_input_weight,
        cross_output_weight,
    )
    going_back = jnp.concatenate([result, back_rows.astype(jnp.bfloat16)], axis=1)
    came_back = lax.all_to_all(going_back, "ev", split_axis=0, concat_axis=0, tiled=True)
    picked = lax.dot_general(
        placement, came_back, (((0,), (0,)), ((), ())), preferred_element_type=jnp.float32
    )
    layer_out = (hidden.astype(jnp.float32) + picked[:, :features]).astype(jnp.bfloat16)
    grad_hidden = (upstream.astype(jnp.float32) + picked[:, features:]).astype(jnp.bfloat16)
    grad_rows = intra_pull(grad_hidden)[0]
    factor = (replicas * owners * local_rows) ** (-0.5)
    partial_sum = jnp.concatenate(
        [
            ordered_contract(normed_half, back_packed, replicas, owners),
            ordered_contract(merged_rows, landed_cotangent, replicas, owners),
        ],
        axis=1,
    )
    portion = reduce_weight_terms(partial_sum, replicas, owners) * factor
    return (
        layer_out[None],
        grad_rows[None],
        portion[:, : 3 * features],
        portion[:, 3 * features :],
    )


def solution(mesh):
    return jax.shard_map(
        on_device,
        mesh=mesh,
        in_specs=(
            P("dp", "ev", None),
            P("dp", "ev", None),
            P(),
            P(),
            P(),
            P(),
            P(),
            P(),
            P("dp", None),
            P("dp", "ev", None, None),
        ),
        out_specs=(P("dp", "ev", None), P("dp", "ev", None), P("ev", None), P("ev", None)),
        check_vma=False,
    )
```

```python
import jax
import jax.numpy as jnp
from jax import lax
from jax.sharding import PartitionSpec as P

HEADS = 8
HEAD_DIM = 64
EVENTS_PER_BLOCK = 128


EPSILON = 1e-05


def layer_norm(values, scale_factors):
    upcast = values.astype(jnp.float32)
    center = upcast - jnp.mean(upcast, axis=-1, keepdims=True)
    spread = jnp.mean(center * center, axis=-1, keepdims=True)
    return center * lax.rsqrt(spread + EPSILON) * scale_factors


def split_heads(matrix, block_groups):
    return matrix.reshape(block_groups, EVENTS_PER_BLOCK, HEADS, HEAD_DIM)


def heads_first(packed_rows, block_groups):
    parts = packed_rows.reshape(block_groups, EVENTS_PER_BLOCK, 3, HEADS, HEAD_DIM)
    return jnp.transpose(parts, (2, 0, 3, 1, 4)).astype(jnp.float32)


def rows_first(merged, row_total):
    return jnp.transpose(merged, (0, 2, 1, 3)).astype(jnp.bfloat16).reshape(row_total, -1)


def intra_branch(source, scale_factors, input_weight, output_weight):
    row_total, features = source.shape
    block_groups = row_total // EVENTS_PER_BLOCK
    normed = layer_norm(source, scale_factors).astype(jnp.bfloat16)
    packed_rows = jnp.dot(normed, input_weight, preferred_element_type=jnp.float32).astype(
        jnp.bfloat16
    )
    parts = heads_first(packed_rows, block_groups)
    queries, key_rows, value_rows = parts[0], parts[1], parts[2]
    scores = jnp.einsum("bhqd,bhkd->bhqk", queries, key_rows) * HEAD_DIM ** (-0.5)
    highest = jnp.max(scores, axis=-1, keepdims=True)
    weights = jnp.exp(scores - highest)
    attention = (weights / jnp.sum(weights, axis=-1, keepdims=True)).astype(jnp.bfloat16)
    merged_rows = jnp.einsum("bhqk,bhkd->bhqd", attention.astype(jnp.float32), value_rows)
    merged_rows = rows_first(merged_rows, row_total)
    branch = jnp.dot(merged_rows, output_weight, preferred_element_type=jnp.float32)
    return (source.astype(jnp.float32) + branch).astype(jnp.bfloat16)


def pick_block(blocks, chosen):
    picked = blocks[0]
    for index in range(1, blocks.shape[0]):
        picked = jnp.where(chosen == index, blocks[index], picked)
    return picked


def gather_segments(blocks, selected_rows, axis):
    block_groups, segments = selected_rows.shape
    return jnp.stack(
        [
            jnp.concatenate(
                [pick_block(blocks, selected_rows[group, segment]) for segment in range(segments)],
                axis=axis,
            )
            for group in range(block_groups)
        ],
        axis=0,
    )


def head_mask(features):
    lanes = jnp.arange(features, dtype=jnp.int32) // HEAD_DIM
    return (lanes[None, :] == jnp.arange(HEADS, dtype=jnp.int32)[:, None]).astype(jnp.float32)


def cross_account_inner(packed_rows, row_presence, block_listing):
    row_total, three_wide = packed_rows.shape
    features = three_wide // 3
    block_groups = row_total // EVENTS_PER_BLOCK
    selected_rows = jnp.concatenate(
        [jnp.arange(block_groups, dtype=jnp.int32)[:, None], block_listing], axis=1
    )
    by_block = packed_rows.astype(jnp.float32).reshape(block_groups, EVENTS_PER_BLOCK, three_wide)
    queries = by_block[:, :, :features]
    key_rows = gather_segments(by_block[:, :, features : 2 * features], selected_rows, 0)
    value_rows = gather_segments(by_block[:, :, 2 * features :], selected_rows, 0)
    presence_blocks = row_presence.reshape(block_groups, EVENTS_PER_BLOCK)
    key_present = gather_segments(presence_blocks, selected_rows, 0)
    key_total = key_present.shape[1]
    itself = (
        jnp.arange(key_total, dtype=jnp.int32)[None, :]
        == jnp.arange(EVENTS_PER_BLOCK, dtype=jnp.int32)[:, None]
    )
    allowed = key_present[:, None, None, :] | itself[None, None, :, :]
    mask = head_mask(features)
    masked_queries = queries[:, None, :, :] * mask[None, :, None, :]
    scores = jnp.einsum("bhqf,bkf->bhqk", masked_queries, key_rows) * HEAD_DIM ** (-0.5)
    scores = jnp.where(allowed, scores, -1e30)
    highest = jnp.max(scores, axis=-1, keepdims=True)
    weights = jnp.where(allowed, jnp.exp(scores - highest), 0.0)
    attention = (weights / jnp.sum(weights, axis=-1, keepdims=True)).astype(jnp.bfloat16)
    per_head = jnp.einsum("bhqk,bkf->bhqf", attention.astype(jnp.float32), value_rows)
    merged_rows = jnp.sum(per_head * mask[None, :, None, :], axis=1)
    return merged_rows.astype(jnp.bfloat16).reshape(row_total, features)


def owner_transfer(
    landed_rows,
    landed_cotangent,
    row_presence,
    block_listing,
    scale_factors,
    input_weight,
    output_weight,
):
    normed, norm_pull = jax.vjp(
        lambda input_operand: layer_norm(input_operand, scale_factors), landed_rows
    )
    normed_half = normed.astype(jnp.bfloat16)
    packed_rows = jnp.dot(normed_half, input_weight, preferred_element_type=jnp.float32).astype(
        jnp.bfloat16
    )
    merged_rows, central_gather = jax.vjp(
        lambda input_operand: cross_account_inner(input_operand, row_presence, block_listing),
        packed_rows,
    )
    result = jnp.dot(merged_rows, output_weight, preferred_element_type=jnp.float32).astype(
        jnp.bfloat16
    )
    back_mixed = lax.dot_general(
        landed_cotangent,
        output_weight,
        (((1,), (1,)), ((), ())),
        preferred_element_type=jnp.float32,
    ).astype(jnp.bfloat16)
    back_packed = central_gather(back_mixed)[0]
    back_normed = lax.dot_general(
        back_packed, input_weight, (((1,), (1,)), ((), ())), preferred_element_type=jnp.float32
    )
    back_rows = norm_pull(back_normed)[0]
    return (result, back_rows, normed_half, back_packed, merged_rows)


def contract(left_part, right_part):
    return lax.dot_general(
        left_part, right_part, (((0,), (0,)), ((), ())), preferred_element_type=jnp.float32
    )


def ordered_contract(left_part, right_part, replicas, owners):
    rows, features = left_part.shape
    per_device = features // owners // replicas
    flipped = jnp.transpose(left_part).reshape(owners, replicas, per_device * rows)
    flipped = jnp.swapaxes(flipped, 0, 1).reshape(features, rows)
    return jnp.dot(flipped, right_part, preferred_element_type=jnp.float32)


def dense_all_to_all(pieces, axis_name):
    count = pieces.shape[0]
    flat = pieces.reshape(count, -1, 128)
    moved = lax.all_to_all(flat, axis_name, 0, 0, tiled=True)
    return moved.reshape(pieces.shape)


def reduce_weight_terms(partial, replicas, owners):
    rows, width = partial.shape
    per_replica = rows // replicas
    per_device = per_replica // owners
    terms = partial.astype(jnp.bfloat16).reshape(replicas, per_replica, width)
    terms = lax.all_to_all(terms, "dp", 0, 0, tiled=True)
    terms = jnp.sum(terms.astype(jnp.float32), axis=0).astype(jnp.bfloat16)
    terms = terms.reshape(owners, per_device, width)
    terms = dense_all_to_all(terms, "ev")
    piece = jnp.sum(terms.astype(jnp.float32), axis=0)
    copies = jnp.broadcast_to(piece[None], (replicas, per_device, width))
    gathered = dense_all_to_all(copies, "dp")
    return gathered.reshape(replicas * per_device, width)


def on_device(
    events,
    cotangent,
    intra_gain,
    intra_proj,
    intra_out,
    cross_norm_gain,
    cross_input_weight,
    cross_output_weight,
    owner_map,
    block_lists,
):
    rows_here = events[0]
    upstream = cotangent[0]
    local_rows, features = rows_here.shape
    owners = lax.axis_size("ev")
    replicas = lax.axis_size("dp")
    own_index = lax.axis_index("ev")
    row_capacity = 2 * local_rows // owners
    buffer_rows = owners * row_capacity
    hidden, intra_pull = jax.vjp(
        lambda input_operand: intra_branch(input_operand, intra_gain, intra_proj, intra_out),
        rows_here,
    )
    targets = owner_map[0]
    onehot = (targets[:, None] == jnp.arange(owners, dtype=jnp.int32)[None, :]).astype(jnp.int32)
    row_counts = jnp.sum(onehot.reshape(owners, local_rows, owners), axis=1)
    inbound_rows = lax.dynamic_index_in_dim(row_counts, own_index, axis=1, keepdims=False)
    own_onehot = lax.dynamic_slice_in_dim(onehot, own_index * local_rows, local_rows, 0)
    before = jnp.cumsum(own_onehot, axis=0) - own_onehot
    slot_ids = jnp.sum(before * own_onehot, axis=1)
    own_dest = lax.dynamic_slice_in_dim(targets, own_index * local_rows, local_rows, 0)
    position = own_dest * row_capacity + slot_ids
    placement = (
        jnp.arange(buffer_rows, dtype=jnp.int32)[:, None] == position[None, :]
    ).astype(jnp.bfloat16)
    both = jnp.concatenate([hidden, upstream], axis=1)
    outgoing = jnp.dot(placement, both, preferred_element_type=jnp.float32).astype(jnp.bfloat16)
    landed = dense_all_to_all(outgoing.reshape(owners, row_capacity, -1), "ev").reshape(
        outgoing.shape
    )
    landed_rows = landed[:, :features]
    landed_cotangent = landed[:, features:]
    row_presence = (
        jnp.arange(row_capacity, dtype=jnp.int32)[None, :] < inbound_rows[:, None]
    ).reshape(buffer_rows)
    block_listing = block_lists[0, 0]
    result, back_rows, normed_half, back_packed, merged_rows = owner_transfer(
        landed_rows,
        landed_cotangent,
        row_presence,
        block_listing,
        cross_norm_gain,
        cross_input_weight,
        cross_output_weight,
    )
    going_back = jnp.concatenate([result, back_rows.astype(jnp.bfloat16)], axis=1)
    came_back = dense_all_to_all(going_back.reshape(owners, row_capacity, -1), "ev").reshape(
        going_back.shape
    )
    picked = lax.dot_general(
        placement, came_back, (((0,), (0,)), ((), ())), preferred_element_type=jnp.float32
    )
    layer_out = (hidden.astype(jnp.float32) + picked[:, :features]).astype(jnp.bfloat16)
    grad_hidden = (upstream.astype(jnp.float32) + picked[:, features:]).astype(jnp.bfloat16)
    grad_rows = intra_pull(grad_hidden)[0]
    factor = (replicas * owners * local_rows) ** (-0.5)
    partial_sum = jnp.concatenate(
        [
            ordered_contract(normed_half, back_packed, replicas, owners),
            ordered_contract(merged_rows, landed_cotangent, replicas, owners),
        ],
        axis=1,
    )
    portion = reduce_weight_terms(partial_sum, replicas, owners) * factor
    return (
        layer_out[None],
        grad_rows[None],
        portion[:, : 3 * features],
        portion[:, 3 * features :],
    )


def solution(mesh):
    return jax.shard_map(
        on_device,
        mesh=mesh,
        in_specs=(
            P("dp", "ev", None),
            P("dp", "ev", None),
            P(),
            P(),
            P(),
            P(),
            P(),
            P(),
            P("dp", None),
            P("dp", "ev", None, None),
        ),
        out_specs=(P("dp", "ev", None), P("dp", "ev", None), P("ev", None), P("ev", None)),
        check_vma=False,
    )
```

```python
import jax
import jax.numpy as jnp
from jax import lax
from jax.sharding import PartitionSpec as P

HEADS = 8
HEAD_DIM = 64
EVENTS_PER_BLOCK = 128


EPSILON = 1e-05


def layer_norm(values, scale_factors):
    upcast = values.astype(jnp.float32)
    center = upcast - jnp.mean(upcast, axis=-1, keepdims=True)
    spread = jnp.mean(center * center, axis=-1, keepdims=True)
    return center * lax.rsqrt(spread + EPSILON) * scale_factors


def split_heads(matrix, block_groups):
    return matrix.reshape(block_groups, EVENTS_PER_BLOCK, HEADS, HEAD_DIM)


def heads_first(packed_rows, block_groups):
    parts = packed_rows.reshape(block_groups, EVENTS_PER_BLOCK, 3, HEADS, HEAD_DIM)
    return jnp.transpose(parts, (2, 0, 3, 1, 4)).astype(jnp.float32)


def rows_first(merged, row_total):
    return jnp.transpose(merged, (0, 2, 1, 3)).astype(jnp.bfloat16).reshape(row_total, -1)


def intra_branch(source, scale_factors, input_weight, output_weight):
    row_total, features = source.shape
    block_groups = row_total // EVENTS_PER_BLOCK
    normed = layer_norm(source, scale_factors).astype(jnp.bfloat16)
    packed_rows = jnp.dot(normed, input_weight, preferred_element_type=jnp.float32).astype(
        jnp.bfloat16
    )
    parts = heads_first(packed_rows, block_groups)
    queries, key_rows, value_rows = parts[0], parts[1], parts[2]
    scores = jnp.einsum("bhqd,bhkd->bhqk", queries, key_rows) * HEAD_DIM ** (-0.5)
    highest = jnp.max(scores, axis=-1, keepdims=True)
    weights = jnp.exp(scores - highest)
    attention = (weights / jnp.sum(weights, axis=-1, keepdims=True)).astype(jnp.bfloat16)
    merged_rows = jnp.einsum("bhqk,bhkd->bhqd", attention.astype(jnp.float32), value_rows)
    merged_rows = rows_first(merged_rows, row_total)
    branch = jnp.dot(merged_rows, output_weight, preferred_element_type=jnp.float32)
    return (source.astype(jnp.float32) + branch).astype(jnp.bfloat16)


def pick_block(blocks, chosen):
    picked = blocks[0]
    for index in range(1, blocks.shape[0]):
        picked = jnp.where(chosen == index, blocks[index], picked)
    return picked


def gather_segments(blocks, selected_rows, axis):
    block_groups, segments = selected_rows.shape
    return jnp.stack(
        [
            jnp.concatenate(
                [pick_block(blocks, selected_rows[group, segment]) for segment in range(segments)],
                axis=axis,
            )
            for group in range(block_groups)
        ],
        axis=0,
    )


def head_mask(features):
    lanes = jnp.arange(features, dtype=jnp.int32) // HEAD_DIM
    return (lanes[None, :] == jnp.arange(HEADS, dtype=jnp.int32)[:, None]).astype(jnp.float32)


def cross_account_inner(packed_rows, row_presence, block_listing):
    row_total, three_wide = packed_rows.shape
    features = three_wide // 3
    block_groups = row_total // EVENTS_PER_BLOCK
    selected_rows = jnp.concatenate(
        [jnp.arange(block_groups, dtype=jnp.int32)[:, None], block_listing], axis=1
    )
    by_block = packed_rows.astype(jnp.float32).reshape(block_groups, EVENTS_PER_BLOCK, three_wide)
    queries = by_block[:, :, :features]
    key_rows = gather_segments(by_block[:, :, features : 2 * features], selected_rows, 0)
    value_rows = gather_segments(by_block[:, :, 2 * features :], selected_rows, 0)
    presence_blocks = row_presence.reshape(block_groups, EVENTS_PER_BLOCK)
    key_present = gather_segments(presence_blocks, selected_rows, 0)
    key_total = key_present.shape[1]
    itself = (
        jnp.arange(key_total, dtype=jnp.int32)[None, :]
        == jnp.arange(EVENTS_PER_BLOCK, dtype=jnp.int32)[:, None]
    )
    allowed = key_present[:, None, None, :] | itself[None, None, :, :]
    mask = head_mask(features)
    masked_queries = queries[:, None, :, :] * mask[None, :, None, :]
    scores = jnp.einsum("bhqf,bkf->bhqk", masked_queries, key_rows) * HEAD_DIM ** (-0.5)
    scores = jnp.where(allowed, scores, -1e30)
    highest = jnp.max(scores, axis=-1, keepdims=True)
    weights = jnp.where(allowed, jnp.exp(scores - highest), 0.0)
    attention = (weights / jnp.sum(weights, axis=-1, keepdims=True)).astype(jnp.bfloat16)
    per_head = jnp.einsum("bhqk,bkf->bhqf", attention.astype(jnp.float32), value_rows)
    merged_rows = jnp.sum(per_head * mask[None, :, None, :], axis=1)
    return merged_rows.astype(jnp.bfloat16).reshape(row_total, features)


def owner_transfer(
    landed_rows,
    landed_cotangent,
    row_presence,
    block_listing,
    scale_factors,
    input_weight,
    output_weight,
):
    normed, norm_pull = jax.vjp(
        lambda input_operand: layer_norm(input_operand, scale_factors), landed_rows
    )
    normed_half = normed.astype(jnp.bfloat16)
    packed_rows = jnp.dot(normed_half, input_weight, preferred_element_type=jnp.float32).astype(
        jnp.bfloat16
    )
    merged_rows, central_gather = jax.vjp(
        lambda input_operand: cross_account_inner(input_operand, row_presence, block_listing),
        packed_rows,
    )
    result = jnp.dot(merged_rows, output_weight, preferred_element_type=jnp.float32).astype(
        jnp.bfloat16
    )
    back_mixed = lax.dot_general(
        landed_cotangent,
        output_weight,
        (((1,), (1,)), ((), ())),
        preferred_element_type=jnp.float32,
    ).astype(jnp.bfloat16)
    back_packed = central_gather(back_mixed)[0]
    back_normed = lax.dot_general(
        back_packed, input_weight, (((1,), (1,)), ((), ())), preferred_element_type=jnp.float32
    )
    back_rows = norm_pull(back_normed)[0]
    return (result, back_rows, normed_half, back_packed, merged_rows)


def contract(left_part, right_part):
    return lax.dot_general(
        left_part, right_part, (((0,), (0,)), ((), ())), preferred_element_type=jnp.float32
    )


def ordered_contract(left_part, right_part, replicas, owners):
    rows, features = left_part.shape
    per_device = features // owners // replicas
    flipped = jnp.transpose(left_part).reshape(owners, replicas, per_device * rows)
    flipped = jnp.swapaxes(flipped, 0, 1).reshape(features, rows)
    return jnp.dot(flipped, right_part, preferred_element_type=jnp.float32)


def dense_all_to_all(pieces, axis_name):
    count = pieces.shape[0]
    flat = pieces.reshape(count, -1, 128)
    moved = lax.all_to_all(flat, axis_name, 0, 0, tiled=True)
    return moved.reshape(pieces.shape)


def replica_sums(partial, replicas):
    rows, width = partial.shape
    terms = partial.astype(jnp.bfloat16).reshape(replicas, rows // replicas, width)
    terms = lax.all_to_all(terms, "dp", 0, 0, tiled=True)
    return jnp.sum(terms.astype(jnp.float32), axis=0).astype(jnp.bfloat16)


def on_device(
    events,
    cotangent,
    intra_gain,
    intra_proj,
    intra_out,
    cross_norm_gain,
    cross_input_weight,
    cross_output_weight,
    owner_map,
    block_lists,
):
    rows_here = events[0]
    upstream = cotangent[0]
    local_rows, features = rows_here.shape
    owners = lax.axis_size("ev")
    replicas = lax.axis_size("dp")
    own_index = lax.axis_index("ev")
    row_capacity = 2 * local_rows // owners
    buffer_rows = owners * row_capacity
    hidden, intra_pull = jax.vjp(
        lambda input_operand: intra_branch(input_operand, intra_gain, intra_proj, intra_out),
        rows_here,
    )
    targets = owner_map[0]
    onehot = (targets[:, None] == jnp.arange(owners, dtype=jnp.int32)[None, :]).astype(jnp.int32)
    row_counts = jnp.sum(onehot.reshape(owners, local_rows, owners), axis=1)
    inbound_rows = lax.dynamic_index_in_dim(row_counts, own_index, axis=1, keepdims=False)
    own_onehot = lax.dynamic_slice_in_dim(onehot, own_index * local_rows, local_rows, 0)
    before = jnp.cumsum(own_onehot, axis=0) - own_onehot
    slot_ids = jnp.sum(before * own_onehot, axis=1)
    own_dest = lax.dynamic_slice_in_dim(targets, own_index * local_rows, local_rows, 0)
    position = own_dest * row_capacity + slot_ids
    placement = (
        jnp.arange(buffer_rows, dtype=jnp.int32)[:, None] == position[None, :]
    ).astype(jnp.bfloat16)
    both = jnp.concatenate([hidden, upstream], axis=1)
    outgoing = jnp.dot(placement, both, preferred_element_type=jnp.float32).astype(jnp.bfloat16)
    landed = dense_all_to_all(outgoing.reshape(owners, row_capacity, -1), "ev").reshape(
        outgoing.shape
    )
    landed_rows = landed[:, :features]
    landed_cotangent = landed[:, features:]
    row_presence = (
        jnp.arange(row_capacity, dtype=jnp.int32)[None, :] < inbound_rows[:, None]
    ).reshape(buffer_rows)
    block_listing = block_lists[0, 0]
    result, back_rows, normed_half, back_packed, merged_rows = owner_transfer(
        landed_rows,
        landed_cotangent,
        row_presence,
        block_listing,
        cross_norm_gain,
        cross_input_weight,
        cross_output_weight,
    )
    factor = (replicas * owners * local_rows) ** (-0.5)
    partial_sum = jnp.concatenate(
        [
            ordered_contract(normed_half, back_packed, replicas, owners),
            ordered_contract(merged_rows, landed_cotangent, replicas, owners),
        ],
        axis=1,
    )
    weight_terms = replica_sums(partial_sum, replicas)
    going_back = jnp.concatenate([result, back_rows.astype(jnp.bfloat16)], axis=1)
    payload = jnp.concatenate(
        [going_back.reshape(owners, -1, 128), weight_terms.reshape(owners, -1, 128)], axis=1
    )
    arrived = lax.all_to_all(payload, "ev", 0, 0, tiled=True)
    split_at = going_back.size // owners // 128
    came_back = arrived[:, :split_at].reshape(going_back.shape)
    owner_terms = arrived[:, split_at:].reshape(owners, -1, weight_terms.shape[1])
    piece = jnp.sum(owner_terms.astype(jnp.float32), axis=0)
    copies = jnp.broadcast_to(piece[None], (replicas,) + piece.shape)
    portion = dense_all_to_all(copies, "dp").reshape(-1, piece.shape[1]) * factor
    picked = lax.dot_general(
        placement, came_back, (((0,), (0,)), ((), ())), preferred_element_type=jnp.float32
    )
    layer_out = (hidden.astype(jnp.float32) + picked[:, :features]).astype(jnp.bfloat16)
    grad_hidden = (upstream.astype(jnp.float32) + picked[:, features:]).astype(jnp.bfloat16)
    grad_rows = intra_pull(grad_hidden)[0]
    return (
        layer_out[None],
        grad_rows[None],
        portion[:, : 3 * features],
        portion[:, 3 * features :],
    )


def solution(mesh):
    return jax.shard_map(
        on_device,
        mesh=mesh,
        in_specs=(
            P("dp", "ev", None),
            P("dp", "ev", None),
            P(),
            P(),
            P(),
            P(),
            P(),
            P(),
            P("dp", None),
            P("dp", "ev", None, None),
        ),
        out_specs=(P("dp", "ev", None), P("dp", "ev", None), P("ev", None), P("ev", None)),
        check_vma=False,
    )
```

```python
import jax
import jax.numpy as jnp
from jax import lax
from jax.sharding import PartitionSpec as P

HEADS = 8
HEAD_DIM = 64
EVENTS_PER_BLOCK = 128


EPSILON = 1e-05


def layer_norm(values, scale_factors):
    upcast = values.astype(jnp.float32)
    center = upcast - jnp.mean(upcast, axis=-1, keepdims=True)
    spread = jnp.mean(center * center, axis=-1, keepdims=True)
    return center * lax.rsqrt(spread + EPSILON) * scale_factors


def split_heads(matrix, block_groups):
    return matrix.reshape(block_groups, EVENTS_PER_BLOCK, HEADS, HEAD_DIM)


def heads_first(packed_rows, block_groups):
    parts = packed_rows.reshape(block_groups, EVENTS_PER_BLOCK, 3, HEADS, HEAD_DIM)
    return jnp.transpose(parts, (2, 0, 3, 1, 4)).astype(jnp.float32)


def rows_first(merged, row_total):
    return jnp.transpose(merged, (0, 2, 1, 3)).astype(jnp.bfloat16).reshape(row_total, -1)


def intra_branch(source, scale_factors, input_weight, output_weight):
    row_total, features = source.shape
    block_groups = row_total // EVENTS_PER_BLOCK
    normed = layer_norm(source, scale_factors).astype(jnp.bfloat16)
    packed_rows = jnp.dot(normed, input_weight, preferred_element_type=jnp.float32).astype(
        jnp.bfloat16
    )
    parts = heads_first(packed_rows, block_groups)
    queries, key_rows, value_rows = parts[0], parts[1], parts[2]
    scores = jnp.einsum("bhqd,bhkd->bhqk", queries, key_rows) * HEAD_DIM ** (-0.5)
    highest = jnp.max(scores, axis=-1, keepdims=True)
    weights = jnp.exp(scores - highest)
    attention = (weights / jnp.sum(weights, axis=-1, keepdims=True)).astype(jnp.bfloat16)
    merged_rows = jnp.einsum("bhqk,bhkd->bhqd", attention.astype(jnp.float32), value_rows)
    merged_rows = rows_first(merged_rows, row_total)
    branch = jnp.dot(merged_rows, output_weight, preferred_element_type=jnp.float32)
    return (source.astype(jnp.float32) + branch).astype(jnp.bfloat16)


def pick_block(blocks, chosen):
    picked = blocks[0]
    for index in range(1, blocks.shape[0]):
        picked = jnp.where(chosen == index, blocks[index], picked)
    return picked


def gather_segments(blocks, selected_rows, axis):
    block_groups, segments = selected_rows.shape
    return jnp.stack(
        [
            jnp.concatenate(
                [pick_block(blocks, selected_rows[group, segment]) for segment in range(segments)],
                axis=axis,
            )
            for group in range(block_groups)
        ],
        axis=0,
    )


def head_mask(features):
    lanes = jnp.arange(features, dtype=jnp.int32) // HEAD_DIM
    return (lanes[None, :] == jnp.arange(HEADS, dtype=jnp.int32)[:, None]).astype(jnp.float32)


def cross_account_inner(packed_rows, row_presence, block_listing):
    row_total, three_wide = packed_rows.shape
    features = three_wide // 3
    block_groups = row_total // EVENTS_PER_BLOCK
    selected_rows = jnp.concatenate(
        [jnp.arange(block_groups, dtype=jnp.int32)[:, None], block_listing], axis=1
    )
    by_block = packed_rows.astype(jnp.float32).reshape(block_groups, EVENTS_PER_BLOCK, three_wide)
    queries = by_block[:, :, :features]
    key_rows = gather_segments(by_block[:, :, features : 2 * features], selected_rows, 0)
    value_rows = gather_segments(by_block[:, :, 2 * features :], selected_rows, 0)
    presence_blocks = row_presence.reshape(block_groups, EVENTS_PER_BLOCK)
    key_present = gather_segments(presence_blocks, selected_rows, 0)
    key_total = key_present.shape[1]
    itself = (
        jnp.arange(key_total, dtype=jnp.int32)[None, :]
        == jnp.arange(EVENTS_PER_BLOCK, dtype=jnp.int32)[:, None]
    )
    allowed = key_present[:, None, None, :] | itself[None, None, :, :]
    mask = head_mask(features)
    masked_queries = queries[:, None, :, :] * mask[None, :, None, :]
    scores = jnp.einsum("bhqf,bkf->bhqk", masked_queries, key_rows) * HEAD_DIM ** (-0.5)
    scores = jnp.where(allowed, scores, -1e30)
    highest = jnp.max(scores, axis=-1, keepdims=True)
    weights = jnp.where(allowed, jnp.exp(scores - highest), 0.0)
    attention = (weights / jnp.sum(weights, axis=-1, keepdims=True)).astype(jnp.bfloat16)
    per_head = jnp.einsum("bhqk,bkf->bhqf", attention.astype(jnp.float32), value_rows)
    merged_rows = jnp.sum(per_head * mask[None, :, None, :], axis=1)
    return merged_rows.astype(jnp.bfloat16).reshape(row_total, features)


def owner_transfer(
    landed_rows,
    landed_cotangent,
    row_presence,
    block_listing,
    scale_factors,
    input_weight,
    output_weight,
):
    normed, norm_pull = jax.vjp(
        lambda input_operand: layer_norm(input_operand, scale_factors), landed_rows
    )
    normed_half = normed.astype(jnp.bfloat16)
    packed_rows = jnp.dot(normed_half, input_weight, preferred_element_type=jnp.float32).astype(
        jnp.bfloat16
    )
    merged_rows, central_gather = jax.vjp(
        lambda input_operand: cross_account_inner(input_operand, row_presence, block_listing),
        packed_rows,
    )
    result = jnp.dot(merged_rows, output_weight, preferred_element_type=jnp.float32).astype(
        jnp.bfloat16
    )
    back_mixed = lax.dot_general(
        landed_cotangent,
        output_weight,
        (((1,), (1,)), ((), ())),
        preferred_element_type=jnp.float32,
    ).astype(jnp.bfloat16)
    back_packed = central_gather(back_mixed)[0]
    back_normed = lax.dot_general(
        back_packed, input_weight, (((1,), (1,)), ((), ())), preferred_element_type=jnp.float32
    )
    back_rows = norm_pull(back_normed)[0]
    return (result, back_rows, normed_half, back_packed, merged_rows)


def contract(left_part, right_part):
    return lax.dot_general(
        left_part, right_part, (((0,), (0,)), ((), ())), preferred_element_type=jnp.float32
    )


def ordered_contract(left_part, right_part, replicas, owners):
    rows, features = left_part.shape
    per_device = features // owners // replicas
    flipped = jnp.transpose(left_part).reshape(owners, replicas, per_device * rows)
    flipped = jnp.swapaxes(flipped, 0, 1).reshape(features, rows)
    return jnp.dot(flipped, right_part, preferred_element_type=jnp.float32)


def dense_all_to_all(pieces, axis_name):
    count = pieces.shape[0]
    flat = pieces.reshape(count, -1, 128)
    moved = lax.all_to_all(flat, axis_name, 0, 0, tiled=True)
    return moved.reshape(pieces.shape)


def reduce_weight_terms(partial, replicas, owners):
    rows, width = partial.shape
    per_device = rows // replicas // owners
    lanes = per_device * width // 128
    terms = partial.astype(jnp.bfloat16).reshape(replicas, owners, lanes, 128)
    terms = lax.all_to_all(terms, "dp", 0, 0, tiled=True)
    terms = jnp.sum(terms.astype(jnp.float32), axis=0).astype(jnp.bfloat16)
    terms = lax.all_to_all(terms, "ev", 0, 0, tiled=True)
    piece = jnp.sum(terms.astype(jnp.float32), axis=0).astype(jnp.bfloat16)
    copies = jnp.broadcast_to(piece[None], (replicas,) + piece.shape)
    gathered = lax.all_to_all(copies, "dp", 0, 0, tiled=True)
    return gathered.reshape(replicas * per_device, width).astype(jnp.float32)


def on_device(
    events,
    cotangent,
    intra_gain,
    intra_proj,
    intra_out,
    cross_norm_gain,
    cross_input_weight,
    cross_output_weight,
    owner_map,
    block_lists,
):
    rows_here = events[0]
    upstream = cotangent[0]
    local_rows, features = rows_here.shape
    owners = lax.axis_size("ev")
    replicas = lax.axis_size("dp")
    own_index = lax.axis_index("ev")
    row_capacity = 2 * local_rows // owners
    buffer_rows = owners * row_capacity
    hidden, intra_pull = jax.vjp(
        lambda input_operand: intra_branch(input_operand, intra_gain, intra_proj, intra_out),
        rows_here,
    )
    targets = owner_map[0]
    onehot = (targets[:, None] == jnp.arange(owners, dtype=jnp.int32)[None, :]).astype(jnp.int32)
    row_counts = jnp.sum(onehot.reshape(owners, local_rows, owners), axis=1)
    inbound_rows = lax.dynamic_index_in_dim(row_counts, own_index, axis=1, keepdims=False)
    own_onehot = lax.dynamic_slice_in_dim(onehot, own_index * local_rows, local_rows, 0)
    before = jnp.cumsum(own_onehot, axis=0) - own_onehot
    slot_ids = jnp.sum(before * own_onehot, axis=1)
    own_dest = lax.dynamic_slice_in_dim(targets, own_index * local_rows, local_rows, 0)
    position = own_dest * row_capacity + slot_ids
    placement = (
        jnp.arange(buffer_rows, dtype=jnp.int32)[:, None] == position[None, :]
    ).astype(jnp.bfloat16)
    both = jnp.concatenate([hidden, upstream], axis=1)
    outgoing = jnp.dot(placement, both, preferred_element_type=jnp.float32).astype(jnp.bfloat16)
    landed = dense_all_to_all(outgoing.reshape(owners, row_capacity, -1), "ev").reshape(
        outgoing.shape
    )
    landed_rows = landed[:, :features]
    landed_cotangent = landed[:, features:]
    row_presence = (
        jnp.arange(row_capacity, dtype=jnp.int32)[None, :] < inbound_rows[:, None]
    ).reshape(buffer_rows)
    block_listing = block_lists[0, 0]
    result, back_rows, normed_half, back_packed, merged_rows = owner_transfer(
        landed_rows,
        landed_cotangent,
        row_presence,
        block_listing,
        cross_norm_gain,
        cross_input_weight,
        cross_output_weight,
    )
    going_back = jnp.concatenate([result, back_rows.astype(jnp.bfloat16)], axis=1)
    came_back = dense_all_to_all(going_back.reshape(owners, row_capacity, -1), "ev").reshape(
        going_back.shape
    )
    picked = lax.dot_general(
        placement, came_back, (((0,), (0,)), ((), ())), preferred_element_type=jnp.float32
    )
    layer_out = (hidden.astype(jnp.float32) + picked[:, :features]).astype(jnp.bfloat16)
    grad_hidden = (upstream.astype(jnp.float32) + picked[:, features:]).astype(jnp.bfloat16)
    grad_rows = intra_pull(grad_hidden)[0]
    factor = (replicas * owners * local_rows) ** (-0.5)
    partial_sum = jnp.concatenate(
        [
            ordered_contract(normed_half, back_packed, replicas, owners),
            ordered_contract(merged_rows, landed_cotangent, replicas, owners),
        ],
        axis=1,
    )
    portion = reduce_weight_terms(partial_sum, replicas, owners) * factor
    return (
        layer_out[None],
        grad_rows[None],
        portion[:, : 3 * features],
        portion[:, 3 * features :],
    )


def solution(mesh):
    return jax.shard_map(
        on_device,
        mesh=mesh,
        in_specs=(
            P("dp", "ev", None),
            P("dp", "ev", None),
            P(),
            P(),
            P(),
            P(),
            P(),
            P(),
            P("dp", None),
            P("dp", "ev", None, None),
        ),
        out_specs=(P("dp", "ev", None), P("dp", "ev", None), P("ev", None), P("ev", None)),
        check_vma=False,
    )
```

```python
import jax
import jax.numpy as jnp
from jax import lax
from jax.sharding import PartitionSpec as P

HEADS = 8
HEAD_DIM = 64
EVENTS_PER_BLOCK = 128


EPSILON = 1e-05


def layer_norm(values, scale_factors):
    upcast = values.astype(jnp.float32)
    center = upcast - jnp.mean(upcast, axis=-1, keepdims=True)
    spread = jnp.mean(center * center, axis=-1, keepdims=True)
    return center * lax.rsqrt(spread + EPSILON) * scale_factors


def split_heads(matrix, block_groups):
    return matrix.reshape(block_groups, EVENTS_PER_BLOCK, HEADS, HEAD_DIM)


def heads_first(packed_rows, block_groups):
    parts = packed_rows.reshape(block_groups, EVENTS_PER_BLOCK, 3, HEADS, HEAD_DIM)
    return jnp.transpose(parts, (2, 0, 3, 1, 4)).astype(jnp.float32)


def rows_first(merged, row_total):
    return jnp.transpose(merged, (0, 2, 1, 3)).astype(jnp.bfloat16).reshape(row_total, -1)


def intra_branch(source, scale_factors, input_weight, output_weight):
    row_total, features = source.shape
    block_groups = row_total // EVENTS_PER_BLOCK
    normed = layer_norm(source, scale_factors).astype(jnp.bfloat16)
    packed_rows = jnp.dot(normed, input_weight, preferred_element_type=jnp.float32).astype(
        jnp.bfloat16
    )
    by_block = packed_rows.astype(jnp.float32).reshape(block_groups, EVENTS_PER_BLOCK, -1)
    queries = by_block[:, :, :features]
    key_rows = by_block[:, :, features : 2 * features]
    value_rows = by_block[:, :, 2 * features :]
    mask = head_mask(features)
    masked_queries = queries[:, None, :, :] * mask[None, :, None, :]
    scores = jnp.einsum("bhqf,bkf->bhqk", masked_queries, key_rows) * HEAD_DIM ** (-0.5)
    highest = jnp.max(scores, axis=-1, keepdims=True)
    weights = jnp.exp(scores - highest)
    attention = (weights / jnp.sum(weights, axis=-1, keepdims=True)).astype(jnp.bfloat16)
    per_head = jnp.einsum("bhqk,bkf->bhqf", attention.astype(jnp.float32), value_rows)
    merged_rows = jnp.sum(per_head * mask[None, :, None, :], axis=1)
    merged_rows = merged_rows.astype(jnp.bfloat16).reshape(row_total, features)
    branch = jnp.dot(merged_rows, output_weight, preferred_element_type=jnp.float32)
    return (source.astype(jnp.float32) + branch).astype(jnp.bfloat16)


def pick_block(blocks, chosen):
    picked = blocks[0]
    for index in range(1, blocks.shape[0]):
        picked = jnp.where(chosen == index, blocks[index], picked)
    return picked


def gather_segments(blocks, selected_rows, axis):
    block_groups, segments = selected_rows.shape
    return jnp.stack(
        [
            jnp.concatenate(
                [pick_block(blocks, selected_rows[group, segment]) for segment in range(segments)],
                axis=axis,
            )
            for group in range(block_groups)
        ],
        axis=0,
    )


def head_mask(features):
    lanes = jnp.arange(features, dtype=jnp.int32) // HEAD_DIM
    return (lanes[None, :] == jnp.arange(HEADS, dtype=jnp.int32)[:, None]).astype(jnp.float32)


def cross_account_inner(packed_rows, row_presence, block_listing):
    row_total, three_wide = packed_rows.shape
    features = three_wide // 3
    block_groups = row_total // EVENTS_PER_BLOCK
    selected_rows = jnp.concatenate(
        [jnp.arange(block_groups, dtype=jnp.int32)[:, None], block_listing], axis=1
    )
    by_block = packed_rows.astype(jnp.float32).reshape(block_groups, EVENTS_PER_BLOCK, three_wide)
    queries = by_block[:, :, :features]
    key_rows = gather_segments(by_block[:, :, features : 2 * features], selected_rows, 0)
    value_rows = gather_segments(by_block[:, :, 2 * features :], selected_rows, 0)
    presence_blocks = row_presence.reshape(block_groups, EVENTS_PER_BLOCK)
    key_present = gather_segments(presence_blocks, selected_rows, 0)
    key_total = key_present.shape[1]
    itself = (
        jnp.arange(key_total, dtype=jnp.int32)[None, :]
        == jnp.arange(EVENTS_PER_BLOCK, dtype=jnp.int32)[:, None]
    )
    allowed = key_present[:, None, None, :] | itself[None, None, :, :]
    mask = head_mask(features)
    masked_queries = queries[:, None, :, :] * mask[None, :, None, :]
    scores = jnp.einsum("bhqf,bkf->bhqk", masked_queries, key_rows) * HEAD_DIM ** (-0.5)
    scores = jnp.where(allowed, scores, -1e30)
    highest = jnp.max(scores, axis=-1, keepdims=True)
    weights = jnp.where(allowed, jnp.exp(scores - highest), 0.0)
    attention = (weights / jnp.sum(weights, axis=-1, keepdims=True)).astype(jnp.bfloat16)
    per_head = jnp.einsum("bhqk,bkf->bhqf", attention.astype(jnp.float32), value_rows)
    merged_rows = jnp.sum(per_head * mask[None, :, None, :], axis=1)
    return merged_rows.astype(jnp.bfloat16).reshape(row_total, features)


def owner_transfer(
    landed_rows,
    landed_cotangent,
    row_presence,
    block_listing,
    scale_factors,
    input_weight,
    output_weight,
):
    normed, norm_pull = jax.vjp(
        lambda input_operand: layer_norm(input_operand, scale_factors), landed_rows
    )
    normed_half = normed.astype(jnp.bfloat16)
    packed_rows = jnp.dot(normed_half, input_weight, preferred_element_type=jnp.float32).astype(
        jnp.bfloat16
    )
    merged_rows, central_gather = jax.vjp(
        lambda input_operand: cross_account_inner(input_operand, row_presence, block_listing),
        packed_rows,
    )
    result = jnp.dot(merged_rows, output_weight, preferred_element_type=jnp.float32).astype(
        jnp.bfloat16
    )
    back_mixed = lax.dot_general(
        landed_cotangent,
        output_weight,
        (((1,), (1,)), ((), ())),
        preferred_element_type=jnp.float32,
    ).astype(jnp.bfloat16)
    back_packed = central_gather(back_mixed)[0]
    back_normed = lax.dot_general(
        back_packed, input_weight, (((1,), (1,)), ((), ())), preferred_element_type=jnp.float32
    )
    back_rows = norm_pull(back_normed)[0]
    return (result, back_rows, normed_half, back_packed, merged_rows)


def contract(left_part, right_part):
    return lax.dot_general(
        left_part, right_part, (((0,), (0,)), ((), ())), preferred_element_type=jnp.float32
    )


def ordered_contract(left_part, right_part, replicas, owners):
    rows, features = left_part.shape
    per_device = features // owners // replicas
    flipped = jnp.transpose(left_part).reshape(owners, replicas, per_device * rows)
    flipped = jnp.swapaxes(flipped, 0, 1).reshape(features, rows)
    return jnp.dot(flipped, right_part, preferred_element_type=jnp.float32)


def dense_all_to_all(pieces, axis_name):
    count = pieces.shape[0]
    flat = pieces.reshape(count, -1, 128)
    moved = lax.all_to_all(flat, axis_name, 0, 0, tiled=True)
    return moved.reshape(pieces.shape)


def reduce_weight_terms(partial, replicas, owners):
    rows, width = partial.shape
    per_replica = rows // replicas
    per_device = per_replica // owners
    terms = partial.astype(jnp.bfloat16).reshape(replicas, per_replica, width)
    terms = lax.all_to_all(terms, "dp", 0, 0, tiled=True)
    terms = jnp.sum(terms.astype(jnp.float32), axis=0).astype(jnp.bfloat16)
    terms = terms.reshape(owners, per_device, width)
    terms = dense_all_to_all(terms, "ev")
    piece = jnp.sum(terms.astype(jnp.float32), axis=0)
    copies = jnp.broadcast_to(piece[None], (replicas, per_device, width))
    gathered = dense_all_to_all(copies, "dp")
    return gathered.reshape(replicas * per_device, width)


def on_device(
    events,
    cotangent,
    intra_gain,
    intra_proj,
    intra_out,
    cross_norm_gain,
    cross_input_weight,
    cross_output_weight,
    owner_map,
    block_lists,
):
    rows_here = events[0]
    upstream = cotangent[0]
    local_rows, features = rows_here.shape
    owners = lax.axis_size("ev")
    replicas = lax.axis_size("dp")
    own_index = lax.axis_index("ev")
    row_capacity = 2 * local_rows // owners
    buffer_rows = owners * row_capacity
    hidden, intra_pull = jax.vjp(
        lambda input_operand: intra_branch(input_operand, intra_gain, intra_proj, intra_out),
        rows_here,
    )
    targets = owner_map[0]
    onehot = (targets[:, None] == jnp.arange(owners, dtype=jnp.int32)[None, :]).astype(jnp.int32)
    row_counts = jnp.sum(onehot.reshape(owners, local_rows, owners), axis=1)
    inbound_rows = lax.dynamic_index_in_dim(row_counts, own_index, axis=1, keepdims=False)
    own_onehot = lax.dynamic_slice_in_dim(onehot, own_index * local_rows, local_rows, 0)
    before = jnp.cumsum(own_onehot, axis=0) - own_onehot
    slot_ids = jnp.sum(before * own_onehot, axis=1)
    own_dest = lax.dynamic_slice_in_dim(targets, own_index * local_rows, local_rows, 0)
    position = own_dest * row_capacity + slot_ids
    placement = (
        jnp.arange(buffer_rows, dtype=jnp.int32)[:, None] == position[None, :]
    ).astype(jnp.bfloat16)
    both = jnp.concatenate([hidden, upstream], axis=1)
    outgoing = jnp.dot(placement, both, preferred_element_type=jnp.float32).astype(jnp.bfloat16)
    landed = dense_all_to_all(outgoing.reshape(owners, row_capacity, -1), "ev").reshape(
        outgoing.shape
    )
    landed_rows = landed[:, :features]
    landed_cotangent = landed[:, features:]
    row_presence = (
        jnp.arange(row_capacity, dtype=jnp.int32)[None, :] < inbound_rows[:, None]
    ).reshape(buffer_rows)
    block_listing = block_lists[0, 0]
    result, back_rows, normed_half, back_packed, merged_rows = owner_transfer(
        landed_rows,
        landed_cotangent,
        row_presence,
        block_listing,
        cross_norm_gain,
        cross_input_weight,
        cross_output_weight,
    )
    going_back = jnp.concatenate([result, back_rows.astype(jnp.bfloat16)], axis=1)
    came_back = dense_all_to_all(going_back.reshape(owners, row_capacity, -1), "ev").reshape(
        going_back.shape
    )
    picked = lax.dot_general(
        placement, came_back, (((0,), (0,)), ((), ())), preferred_element_type=jnp.float32
    )
    layer_out = (hidden.astype(jnp.float32) + picked[:, :features]).astype(jnp.bfloat16)
    grad_hidden = (upstream.astype(jnp.float32) + picked[:, features:]).astype(jnp.bfloat16)
    grad_rows = intra_pull(grad_hidden)[0]
    factor = (replicas * owners * local_rows) ** (-0.5)
    partial_sum = jnp.concatenate(
        [
            ordered_contract(normed_half, back_packed, replicas, owners),
            ordered_contract(merged_rows, landed_cotangent, replicas, owners),
        ],
        axis=1,
    )
    portion = reduce_weight_terms(partial_sum, replicas, owners) * factor
    return (
        layer_out[None],
        grad_rows[None],
        portion[:, : 3 * features],
        portion[:, 3 * features :],
    )


def solution(mesh):
    return jax.shard_map(
        on_device,
        mesh=mesh,
        in_specs=(
            P("dp", "ev", None),
            P("dp", "ev", None),
            P(),
            P(),
            P(),
            P(),
            P(),
            P(),
            P("dp", None),
            P("dp", "ev", None, None),
        ),
        out_specs=(P("dp", "ev", None), P("dp", "ev", None), P("ev", None), P("ev", None)),
        check_vma=False,
    )
```

```python
import jax
import jax.numpy as jnp
from jax import lax
from jax.sharding import PartitionSpec as P

HEADS = 8
HEAD_DIM = 64
EVENTS_PER_BLOCK = 128


EPSILON = 1e-05


def layer_norm(values, scale_factors):
    upcast = values.astype(jnp.float32)
    center = upcast - jnp.mean(upcast, axis=-1, keepdims=True)
    spread = jnp.mean(center * center, axis=-1, keepdims=True)
    return center * lax.rsqrt(spread + EPSILON) * scale_factors


def split_heads(matrix, block_groups):
    return matrix.reshape(block_groups, EVENTS_PER_BLOCK, HEADS, HEAD_DIM)


def heads_first(packed_rows, block_groups):
    parts = packed_rows.reshape(block_groups, EVENTS_PER_BLOCK, 3, HEADS, HEAD_DIM)
    return jnp.transpose(parts, (2, 0, 3, 1, 4)).astype(jnp.float32)


def rows_first(merged, row_total):
    return jnp.transpose(merged, (0, 2, 1, 3)).astype(jnp.bfloat16).reshape(row_total, -1)


def intra_branch(source, scale_factors, input_weight, output_weight):
    row_total, features = source.shape
    block_groups = row_total // EVENTS_PER_BLOCK
    normed = layer_norm(source, scale_factors).astype(jnp.bfloat16)
    packed_rows = jnp.dot(normed, input_weight, preferred_element_type=jnp.float32).astype(
        jnp.bfloat16
    )
    by_block = packed_rows.astype(jnp.float32).reshape(block_groups, EVENTS_PER_BLOCK, -1)
    queries = by_block[:, :, :features]
    key_rows = by_block[:, :, features : 2 * features]
    value_rows = by_block[:, :, 2 * features :]
    mask = head_mask(features)
    masked_queries = queries[:, None, :, :] * mask[None, :, None, :]
    scores = jnp.einsum("bhqf,bkf->bhqk", masked_queries, key_rows) * HEAD_DIM ** (-0.5)
    highest = jnp.max(scores, axis=-1, keepdims=True)
    weights = jnp.exp(scores - highest)
    attention = (weights / jnp.sum(weights, axis=-1, keepdims=True)).astype(jnp.bfloat16)
    per_head = jnp.einsum("bhqk,bkf->bhqf", attention.astype(jnp.float32), value_rows)
    merged_rows = jnp.sum(per_head * mask[None, :, None, :], axis=1)
    merged_rows = merged_rows.astype(jnp.bfloat16).reshape(row_total, features)
    branch = jnp.dot(merged_rows, output_weight, preferred_element_type=jnp.float32)
    return (source.astype(jnp.float32) + branch).astype(jnp.bfloat16)


def pick_block(blocks, chosen):
    picked = blocks[0]
    for index in range(1, blocks.shape[0]):
        picked = jnp.where(chosen == index, blocks[index], picked)
    return picked


def gather_segments(blocks, selected_rows, axis):
    block_groups, segments = selected_rows.shape
    return jnp.stack(
        [
            jnp.concatenate(
                [pick_block(blocks, selected_rows[group, segment]) for segment in range(segments)],
                axis=axis,
            )
            for group in range(block_groups)
        ],
        axis=0,
    )


def head_mask(features):
    lanes = jnp.arange(features, dtype=jnp.int32) // HEAD_DIM
    return (lanes[None, :] == jnp.arange(HEADS, dtype=jnp.int32)[:, None]).astype(jnp.float32)


def cross_account_inner(packed_rows, row_presence, block_listing):
    row_total, three_wide = packed_rows.shape
    features = three_wide // 3
    block_groups = row_total // EVENTS_PER_BLOCK
    selected_rows = jnp.concatenate(
        [jnp.arange(block_groups, dtype=jnp.int32)[:, None], block_listing], axis=1
    )
    by_block = packed_rows.astype(jnp.float32).reshape(block_groups, EVENTS_PER_BLOCK, three_wide)
    queries = by_block[:, :, :features]
    key_rows = gather_segments(by_block[:, :, features : 2 * features], selected_rows, 0)
    value_rows = gather_segments(by_block[:, :, 2 * features :], selected_rows, 0)
    presence_blocks = row_presence.reshape(block_groups, EVENTS_PER_BLOCK)
    key_present = gather_segments(presence_blocks, selected_rows, 0)
    key_total = key_present.shape[1]
    itself = (
        jnp.arange(key_total, dtype=jnp.int32)[None, :]
        == jnp.arange(EVENTS_PER_BLOCK, dtype=jnp.int32)[:, None]
    )
    allowed = key_present[:, None, None, :] | itself[None, None, :, :]
    mask = head_mask(features)
    masked_queries = queries[:, None, :, :] * mask[None, :, None, :]
    scores = jnp.einsum("bhqf,bkf->bhqk", masked_queries, key_rows) * HEAD_DIM ** (-0.5)
    scores = jnp.where(allowed, scores, -1e30)
    highest = jnp.max(scores, axis=-1, keepdims=True)
    weights = jnp.where(allowed, jnp.exp(scores - highest), 0.0)
    attention = (weights / jnp.sum(weights, axis=-1, keepdims=True)).astype(jnp.bfloat16)
    per_head = jnp.einsum("bhqk,bkf->bhqf", attention.astype(jnp.float32), value_rows)
    merged_rows = jnp.sum(per_head * mask[None, :, None, :], axis=1)
    return merged_rows.astype(jnp.bfloat16).reshape(row_total, features)


def owner_transfer(
    landed_rows,
    landed_cotangent,
    row_presence,
    block_listing,
    scale_factors,
    input_weight,
    output_weight,
):
    normed, norm_pull = jax.vjp(
        lambda input_operand: layer_norm(input_operand, scale_factors), landed_rows
    )
    normed_half = normed.astype(jnp.bfloat16)
    packed_rows = jnp.dot(normed_half, input_weight, preferred_element_type=jnp.float32).astype(
        jnp.bfloat16
    )
    merged_rows, central_gather = jax.vjp(
        lambda input_operand: cross_account_inner(input_operand, row_presence, block_listing),
        packed_rows,
    )
    result = jnp.dot(merged_rows, output_weight, preferred_element_type=jnp.float32).astype(
        jnp.bfloat16
    )
    back_mixed = lax.dot_general(
        landed_cotangent,
        output_weight,
        (((1,), (1,)), ((), ())),
        preferred_element_type=jnp.float32,
    ).astype(jnp.bfloat16)
    back_packed = central_gather(back_mixed)[0]
    back_normed = lax.dot_general(
        back_packed, input_weight, (((1,), (1,)), ((), ())), preferred_element_type=jnp.float32
    )
    back_rows = norm_pull(back_normed)[0]
    return (result, back_rows, normed_half, back_packed, merged_rows)


def contract(left_part, right_part):
    return lax.dot_general(
        left_part, right_part, (((0,), (0,)), ((), ())), preferred_element_type=jnp.float32
    )


def ordered_contract(left_part, right_part, replicas, owners):
    rows, features = left_part.shape
    per_device = features // owners // replicas
    flipped = jnp.transpose(left_part).reshape(owners, replicas, per_device * rows)
    flipped = jnp.swapaxes(flipped, 0, 1).reshape(features, rows)
    return jnp.dot(flipped, right_part, preferred_element_type=jnp.float32)


def dense_all_to_all(pieces, axis_name):
    count = pieces.shape[0]
    flat = pieces.reshape(count, -1, 128)
    moved = lax.all_to_all(flat, axis_name, 0, 0, tiled=True)
    return moved.reshape(pieces.shape)


def reduce_weight_terms(partial, replicas, owners):
    rows, width = partial.shape
    per_replica = rows // replicas
    per_device = per_replica // owners
    terms = partial.astype(jnp.bfloat16).reshape(replicas, per_replica, width)
    terms = lax.all_to_all(terms, "dp", 0, 0, tiled=True)
    terms = jnp.sum(terms.astype(jnp.float32), axis=0).astype(jnp.bfloat16)
    terms = terms.reshape(owners, per_device, width)
    terms = dense_all_to_all(terms, "ev")
    piece = jnp.sum(terms.astype(jnp.float32), axis=0)
    copies = jnp.broadcast_to(piece[None], (replicas, per_device, width))
    gathered = dense_all_to_all(copies, "dp")
    return gathered.reshape(replicas * per_device, width)


def on_device(
    events,
    cotangent,
    intra_gain,
    intra_proj,
    intra_out,
    cross_norm_gain,
    cross_input_weight,
    cross_output_weight,
    owner_map,
    block_lists,
):
    rows_here = events[0]
    upstream = cotangent[0]
    local_rows, features = rows_here.shape
    owners = lax.axis_size("ev")
    replicas = lax.axis_size("dp")
    own_index = lax.axis_index("ev")
    row_capacity = 2 * local_rows // owners
    buffer_rows = owners * row_capacity
    hidden, intra_pull = jax.vjp(
        lambda input_operand: intra_branch(input_operand, intra_gain, intra_proj, intra_out),
        rows_here,
    )
    targets = owner_map[0]
    own_dest = lax.dynamic_slice_in_dim(targets, own_index * local_rows, local_rows, 0)
    owner_ids = jnp.arange(owners, dtype=jnp.int32)
    own_onehot = (own_dest[:, None] == owner_ids[None, :]).astype(jnp.int32)
    before = jnp.cumsum(own_onehot, axis=0) - own_onehot
    slot_ids = jnp.sum(before * own_onehot, axis=1)
    inbound_rows = jnp.sum((targets == own_index).astype(jnp.int32).reshape(owners, local_rows), axis=1)
    position = own_dest * row_capacity + slot_ids
    placement = (
        jnp.arange(buffer_rows, dtype=jnp.int32)[:, None] == position[None, :]
    ).astype(jnp.bfloat16)
    both = jnp.concatenate([hidden, upstream], axis=1)
    outgoing = jnp.dot(placement, both, preferred_element_type=jnp.float32).astype(jnp.bfloat16)
    landed = dense_all_to_all(outgoing.reshape(owners, row_capacity, -1), "ev").reshape(
        outgoing.shape
    )
    landed_rows = landed[:, :features]
    landed_cotangent = landed[:, features:]
    row_presence = (
        jnp.arange(row_capacity, dtype=jnp.int32)[None, :] < inbound_rows[:, None]
    ).reshape(buffer_rows)
    block_listing = block_lists[0, 0]
    result, back_rows, normed_half, back_packed, merged_rows = owner_transfer(
        landed_rows,
        landed_cotangent,
        row_presence,
        block_listing,
        cross_norm_gain,
        cross_input_weight,
        cross_output_weight,
    )
    going_back = jnp.concatenate([result, back_rows.astype(jnp.bfloat16)], axis=1)
    came_back = dense_all_to_all(going_back.reshape(owners, row_capacity, -1), "ev").reshape(
        going_back.shape
    )
    picked = lax.dot_general(
        placement, came_back, (((0,), (0,)), ((), ())), preferred_element_type=jnp.float32
    )
    layer_out = (hidden.astype(jnp.float32) + picked[:, :features]).astype(jnp.bfloat16)
    grad_hidden = (upstream.astype(jnp.float32) + picked[:, features:]).astype(jnp.bfloat16)
    grad_rows = intra_pull(grad_hidden)[0]
    factor = (replicas * owners * local_rows) ** (-0.5)
    partial_sum = jnp.concatenate(
        [
            ordered_contract(normed_half, back_packed, replicas, owners),
            ordered_contract(merged_rows, landed_cotangent, replicas, owners),
        ],
        axis=1,
    )
    portion = reduce_weight_terms(partial_sum, replicas, owners) * factor
    return (
        layer_out[None],
        grad_rows[None],
        portion[:, : 3 * features],
        portion[:, 3 * features :],
    )


def solution(mesh):
    return jax.shard_map(
        on_device,
        mesh=mesh,
        in_specs=(
            P("dp", "ev", None),
            P("dp", "ev", None),
            P(),
            P(),
            P(),
            P(),
            P(),
            P(),
            P("dp", None),
            P("dp", "ev", None, None),
        ),
        out_specs=(P("dp", "ev", None), P("dp", "ev", None), P("ev", None), P("ev", None)),
        check_vma=False,
    )
```

```python
import jax
import jax.numpy as jnp
from jax import lax
from jax.sharding import PartitionSpec as P

HEADS = 8
HEAD_DIM = 64
EVENTS_PER_BLOCK = 128


EPSILON = 1e-05


def layer_norm(values, scale_factors):
    upcast = values.astype(jnp.float32)
    center = upcast - jnp.mean(upcast, axis=-1, keepdims=True)
    spread = jnp.mean(center * center, axis=-1, keepdims=True)
    return center * lax.rsqrt(spread + EPSILON) * scale_factors


def split_heads(matrix, block_groups):
    return matrix.reshape(block_groups, EVENTS_PER_BLOCK, HEADS, HEAD_DIM)


def heads_first(packed_rows, block_groups):
    parts = packed_rows.reshape(block_groups, EVENTS_PER_BLOCK, 3, HEADS, HEAD_DIM)
    return jnp.transpose(parts, (2, 0, 3, 1, 4)).astype(jnp.float32)


def rows_first(merged, row_total):
    return jnp.transpose(merged, (0, 2, 1, 3)).astype(jnp.bfloat16).reshape(row_total, -1)


def intra_branch(source, scale_factors, input_weight, output_weight):
    row_total, features = source.shape
    block_groups = row_total // EVENTS_PER_BLOCK
    normed = layer_norm(source, scale_factors).astype(jnp.bfloat16)
    packed_rows = jnp.dot(normed, input_weight, preferred_element_type=jnp.float32).astype(
        jnp.bfloat16
    )
    by_block = packed_rows.astype(jnp.float32).reshape(block_groups, EVENTS_PER_BLOCK, -1)
    queries = by_block[:, :, :features]
    key_rows = by_block[:, :, features : 2 * features]
    value_rows = by_block[:, :, 2 * features :]
    mask = head_mask(features)
    masked_queries = queries[:, None, :, :] * mask[None, :, None, :]
    scores = jnp.einsum("bhqf,bkf->bhqk", masked_queries, key_rows) * HEAD_DIM ** (-0.5)
    highest = jnp.max(scores, axis=-1, keepdims=True)
    weights = jnp.exp(scores - highest)
    attention = (weights / jnp.sum(weights, axis=-1, keepdims=True)).astype(jnp.bfloat16)
    per_head = jnp.einsum("bhqk,bkf->bhqf", attention.astype(jnp.float32), value_rows)
    merged_rows = jnp.sum(per_head * mask[None, :, None, :], axis=1)
    merged_rows = merged_rows.astype(jnp.bfloat16).reshape(row_total, features)
    branch = jnp.dot(merged_rows, output_weight, preferred_element_type=jnp.float32)
    return (source.astype(jnp.float32) + branch).astype(jnp.bfloat16)


def pick_block(blocks, chosen):
    picked = blocks[0]
    for index in range(1, blocks.shape[0]):
        picked = jnp.where(chosen == index, blocks[index], picked)
    return picked


def gather_segments(blocks, selected_rows, axis):
    block_groups, segments = selected_rows.shape
    return jnp.stack(
        [
            jnp.concatenate(
                [pick_block(blocks, selected_rows[group, segment]) for segment in range(segments)],
                axis=axis,
            )
            for group in range(block_groups)
        ],
        axis=0,
    )


def head_mask(features):
    lanes = jnp.arange(features, dtype=jnp.int32) // HEAD_DIM
    return (lanes[None, :] == jnp.arange(HEADS, dtype=jnp.int32)[:, None]).astype(jnp.float32)


def cross_account_inner(packed_rows, row_presence, block_listing):
    row_total, three_wide = packed_rows.shape
    features = three_wide // 3
    block_groups = row_total // EVENTS_PER_BLOCK
    selected_rows = jnp.concatenate(
        [jnp.arange(block_groups, dtype=jnp.int32)[:, None], block_listing], axis=1
    )
    by_block = packed_rows.astype(jnp.float32).reshape(block_groups, EVENTS_PER_BLOCK, three_wide)
    queries = by_block[:, :, :features]
    key_rows = gather_segments(by_block[:, :, features : 2 * features], selected_rows, 0)
    value_rows = gather_segments(by_block[:, :, 2 * features :], selected_rows, 0)
    presence_blocks = row_presence.reshape(block_groups, EVENTS_PER_BLOCK)
    key_present = gather_segments(presence_blocks, selected_rows, 0)
    key_total = key_present.shape[1]
    itself = (
        jnp.arange(key_total, dtype=jnp.int32)[None, :]
        == jnp.arange(EVENTS_PER_BLOCK, dtype=jnp.int32)[:, None]
    )
    allowed = key_present[:, None, None, :] | itself[None, None, :, :]
    mask = head_mask(features)
    masked_queries = queries[:, None, :, :] * mask[None, :, None, :]
    scores = jnp.einsum("bhqf,bkf->bhqk", masked_queries, key_rows) * HEAD_DIM ** (-0.5)
    scores = jnp.where(allowed, scores, -1e30)
    highest = jnp.max(scores, axis=-1, keepdims=True)
    weights = jnp.where(allowed, jnp.exp(scores - highest), 0.0)
    attention = (weights / jnp.sum(weights, axis=-1, keepdims=True)).astype(jnp.bfloat16)
    per_head = jnp.einsum("bhqk,bkf->bhqf", attention.astype(jnp.float32), value_rows)
    merged_rows = jnp.sum(per_head * mask[None, :, None, :], axis=1)
    return merged_rows.astype(jnp.bfloat16).reshape(row_total, features)


def owner_transfer(
    landed_rows,
    landed_cotangent,
    row_presence,
    block_listing,
    scale_factors,
    input_weight,
    output_weight,
):
    normed, norm_pull = jax.vjp(
        lambda input_operand: layer_norm(input_operand, scale_factors), landed_rows
    )
    normed_half = normed.astype(jnp.bfloat16)
    packed_rows = jnp.dot(normed_half, input_weight, preferred_element_type=jnp.float32).astype(
        jnp.bfloat16
    )
    merged_rows, central_gather = jax.vjp(
        lambda input_operand: cross_account_inner(input_operand, row_presence, block_listing),
        packed_rows,
    )
    result = jnp.dot(merged_rows, output_weight, preferred_element_type=jnp.float32).astype(
        jnp.bfloat16
    )
    back_mixed = lax.dot_general(
        landed_cotangent,
        output_weight,
        (((1,), (1,)), ((), ())),
        preferred_element_type=jnp.float32,
    ).astype(jnp.bfloat16)
    back_packed = central_gather(back_mixed)[0]
    back_normed = lax.dot_general(
        back_packed, input_weight, (((1,), (1,)), ((), ())), preferred_element_type=jnp.float32
    )
    back_rows = norm_pull(back_normed)[0]
    return (result, back_rows, normed_half, back_packed, merged_rows)


def contract(left_part, right_part):
    return lax.dot_general(
        left_part, right_part, (((0,), (0,)), ((), ())), preferred_element_type=jnp.float32
    )


def ordered_contract(left_part, right_part, replicas, owners):
    rows, features = left_part.shape
    per_device = features // owners // replicas
    flipped = jnp.transpose(left_part).reshape(owners, replicas, per_device * rows)
    flipped = jnp.swapaxes(flipped, 0, 1).reshape(features, rows)
    return jnp.dot(flipped, right_part, preferred_element_type=jnp.float32)


def dense_all_to_all(pieces, axis_name):
    count = pieces.shape[0]
    flat = pieces.reshape(count, -1, 128)
    moved = lax.all_to_all(flat, axis_name, 0, 0, tiled=True)
    return moved.reshape(pieces.shape)


def reduce_weight_terms(partial, replicas, owners):
    rows, width = partial.shape
    per_replica = rows // replicas
    per_device = per_replica // owners
    terms = partial.astype(jnp.bfloat16).reshape(replicas, per_replica, width)
    terms = lax.all_to_all(terms, "dp", 0, 0, tiled=True)
    terms = jnp.sum(terms.astype(jnp.float32), axis=0).astype(jnp.bfloat16)
    terms = terms.reshape(owners, per_device, width)
    terms = dense_all_to_all(terms, "ev")
    piece = jnp.sum(terms.astype(jnp.float32), axis=0).astype(jnp.bfloat16)
    copies = jnp.broadcast_to(piece[None], (replicas, per_device, width))
    gathered = dense_all_to_all(copies, "dp")
    return gathered.reshape(replicas * per_device, width).astype(jnp.float32)


def on_device(
    events,
    cotangent,
    intra_gain,
    intra_proj,
    intra_out,
    cross_norm_gain,
    cross_input_weight,
    cross_output_weight,
    owner_map,
    block_lists,
):
    rows_here = events[0]
    upstream = cotangent[0]
    local_rows, features = rows_here.shape
    owners = lax.axis_size("ev")
    replicas = lax.axis_size("dp")
    own_index = lax.axis_index("ev")
    row_capacity = 2 * local_rows // owners
    buffer_rows = owners * row_capacity
    hidden, intra_pull = jax.vjp(
        lambda input_operand: intra_branch(input_operand, intra_gain, intra_proj, intra_out),
        rows_here,
    )
    targets = owner_map[0]
    onehot = (targets[:, None] == jnp.arange(owners, dtype=jnp.int32)[None, :]).astype(jnp.int32)
    row_counts = jnp.sum(onehot.reshape(owners, local_rows, owners), axis=1)
    inbound_rows = lax.dynamic_index_in_dim(row_counts, own_index, axis=1, keepdims=False)
    own_onehot = lax.dynamic_slice_in_dim(onehot, own_index * local_rows, local_rows, 0)
    before = jnp.cumsum(own_onehot, axis=0) - own_onehot
    slot_ids = jnp.sum(before * own_onehot, axis=1)
    own_dest = lax.dynamic_slice_in_dim(targets, own_index * local_rows, local_rows, 0)
    position = own_dest * row_capacity + slot_ids
    placement = (
        jnp.arange(buffer_rows, dtype=jnp.int32)[:, None] == position[None, :]
    ).astype(jnp.bfloat16)
    both = jnp.concatenate([hidden, upstream], axis=1)
    outgoing = jnp.dot(placement, both, preferred_element_type=jnp.float32).astype(jnp.bfloat16)
    landed = dense_all_to_all(outgoing.reshape(owners, row_capacity, -1), "ev").reshape(
        outgoing.shape
    )
    landed_rows = landed[:, :features]
    landed_cotangent = landed[:, features:]
    row_presence = (
        jnp.arange(row_capacity, dtype=jnp.int32)[None, :] < inbound_rows[:, None]
    ).reshape(buffer_rows)
    block_listing = block_lists[0, 0]
    result, back_rows, normed_half, back_packed, merged_rows = owner_transfer(
        landed_rows,
        landed_cotangent,
        row_presence,
        block_listing,
        cross_norm_gain,
        cross_input_weight,
        cross_output_weight,
    )
    going_back = jnp.concatenate([result, back_rows.astype(jnp.bfloat16)], axis=1)
    came_back = dense_all_to_all(going_back.reshape(owners, row_capacity, -1), "ev").reshape(
        going_back.shape
    )
    picked = lax.dot_general(
        placement, came_back, (((0,), (0,)), ((), ())), preferred_element_type=jnp.float32
    )
    layer_out = (hidden.astype(jnp.float32) + picked[:, :features]).astype(jnp.bfloat16)
    grad_hidden = (upstream.astype(jnp.float32) + picked[:, features:]).astype(jnp.bfloat16)
    grad_rows = intra_pull(grad_hidden)[0]
    factor = (replicas * owners * local_rows) ** (-0.5)
    partial_sum = jnp.concatenate(
        [
            ordered_contract(normed_half, back_packed, replicas, owners),
            ordered_contract(merged_rows, landed_cotangent, replicas, owners),
        ],
        axis=1,
    )
    portion = reduce_weight_terms(partial_sum, replicas, owners) * factor
    return (
        layer_out[None],
        grad_rows[None],
        portion[:, : 3 * features],
        portion[:, 3 * features :],
    )


def solution(mesh):
    return jax.shard_map(
        on_device,
        mesh=mesh,
        in_specs=(
            P("dp", "ev", None),
            P("dp", "ev", None),
            P(),
            P(),
            P(),
            P(),
            P(),
            P(),
            P("dp", None),
            P("dp", "ev", None, None),
        ),
        out_specs=(P("dp", "ev", None), P("dp", "ev", None), P("ev", None), P("ev", None)),
        check_vma=False,
    )
```

```python
import jax
import jax.numpy as jnp
from jax import lax
from jax.sharding import PartitionSpec as P

HEADS = 8
HEAD_DIM = 64
EVENTS_PER_BLOCK = 128


EPSILON = 1e-05


def layer_norm(values, scale_factors):
    upcast = values.astype(jnp.float32)
    center = upcast - jnp.mean(upcast, axis=-1, keepdims=True)
    spread = jnp.mean(center * center, axis=-1, keepdims=True)
    return center * lax.rsqrt(spread + EPSILON) * scale_factors


def split_heads(matrix, block_groups):
    return matrix.reshape(block_groups, EVENTS_PER_BLOCK, HEADS, HEAD_DIM)


def heads_first(packed_rows, block_groups):
    parts = packed_rows.reshape(block_groups, EVENTS_PER_BLOCK, 3, HEADS, HEAD_DIM)
    return jnp.transpose(parts, (2, 0, 3, 1, 4)).astype(jnp.float32)


def rows_first(merged, row_total):
    return jnp.transpose(merged, (0, 2, 1, 3)).astype(jnp.bfloat16).reshape(row_total, -1)


def intra_branch(source, scale_factors, input_weight, output_weight):
    row_total, features = source.shape
    block_groups = row_total // EVENTS_PER_BLOCK
    normed = layer_norm(source, scale_factors).astype(jnp.bfloat16)
    packed_rows = jnp.dot(normed, input_weight, preferred_element_type=jnp.float32).astype(
        jnp.bfloat16
    )
    by_block = packed_rows.astype(jnp.float32).reshape(block_groups, EVENTS_PER_BLOCK, -1)
    queries = by_block[:, :, :features]
    key_rows = by_block[:, :, features : 2 * features]
    value_rows = by_block[:, :, 2 * features :]
    mask = head_mask(features)
    masked_queries = queries[:, None, :, :] * mask[None, :, None, :]
    scores = jnp.einsum("bhqf,bkf->bhqk", masked_queries, key_rows) * HEAD_DIM ** (-0.5)
    highest = jnp.max(scores, axis=-1, keepdims=True)
    weights = jnp.exp(scores - highest)
    attention = (weights / jnp.sum(weights, axis=-1, keepdims=True)).astype(jnp.bfloat16)
    per_head = jnp.einsum("bhqk,bkf->bhqf", attention.astype(jnp.float32), value_rows)
    merged_rows = jnp.sum(per_head * mask[None, :, None, :], axis=1)
    merged_rows = merged_rows.astype(jnp.bfloat16).reshape(row_total, features)
    branch = jnp.dot(merged_rows, output_weight, preferred_element_type=jnp.float32)
    return (source.astype(jnp.float32) + branch).astype(jnp.bfloat16)


def pick_block(blocks, chosen):
    picked = blocks[0]
    for index in range(1, blocks.shape[0]):
        picked = jnp.where(chosen == index, blocks[index], picked)
    return picked


def gather_segments(blocks, selected_rows, axis):
    block_groups, segments = selected_rows.shape
    return jnp.stack(
        [
            jnp.concatenate(
                [pick_block(blocks, selected_rows[group, segment]) for segment in range(segments)],
                axis=axis,
            )
            for group in range(block_groups)
        ],
        axis=0,
    )


def head_mask(features):
    lanes = jnp.arange(features, dtype=jnp.int32) // HEAD_DIM
    return (lanes[None, :] == jnp.arange(HEADS, dtype=jnp.int32)[:, None]).astype(jnp.float32)


def cross_account_inner(packed_rows, row_presence, block_listing):
    row_total, three_wide = packed_rows.shape
    features = three_wide // 3
    block_groups = row_total // EVENTS_PER_BLOCK
    selected_rows = jnp.concatenate(
        [jnp.arange(block_groups, dtype=jnp.int32)[:, None], block_listing], axis=1
    )
    by_block = packed_rows.astype(jnp.float32).reshape(block_groups, EVENTS_PER_BLOCK, three_wide)
    queries = by_block[:, :, :features]
    key_rows = gather_segments(by_block[:, :, features : 2 * features], selected_rows, 0)
    value_rows = gather_segments(by_block[:, :, 2 * features :], selected_rows, 0)
    presence_blocks = row_presence.reshape(block_groups, EVENTS_PER_BLOCK)
    key_present = gather_segments(presence_blocks, selected_rows, 0)
    key_total = key_present.shape[1]
    itself = (
        jnp.arange(key_total, dtype=jnp.int32)[None, :]
        == jnp.arange(EVENTS_PER_BLOCK, dtype=jnp.int32)[:, None]
    )
    allowed = key_present[:, None, None, :] | itself[None, None, :, :]
    mask = head_mask(features)
    masked_queries = queries[:, None, :, :] * mask[None, :, None, :]
    scores = jnp.einsum("bhqf,bkf->bhqk", masked_queries, key_rows) * HEAD_DIM ** (-0.5)
    scores = jnp.where(allowed, scores, -1e30)
    highest = jnp.max(scores, axis=-1, keepdims=True)
    weights = jnp.where(allowed, jnp.exp(scores - highest), 0.0)
    attention = (weights / jnp.sum(weights, axis=-1, keepdims=True)).astype(jnp.bfloat16)
    per_head = jnp.einsum("bhqk,bkf->bhqf", attention.astype(jnp.float32), value_rows)
    merged_rows = jnp.sum(per_head * mask[None, :, None, :], axis=1)
    return merged_rows.astype(jnp.bfloat16).reshape(row_total, features)


def owner_transfer(
    landed_rows,
    landed_cotangent,
    row_presence,
    block_listing,
    scale_factors,
    input_weight,
    output_weight,
):
    normed, norm_pull = jax.vjp(
        lambda input_operand: layer_norm(input_operand, scale_factors), landed_rows
    )
    normed_half = normed.astype(jnp.bfloat16)
    packed_rows = jnp.dot(normed_half, input_weight, preferred_element_type=jnp.float32).astype(
        jnp.bfloat16
    )
    merged_rows, central_gather = jax.vjp(
        lambda input_operand: cross_account_inner(input_operand, row_presence, block_listing),
        packed_rows,
    )
    result = jnp.dot(merged_rows, output_weight, preferred_element_type=jnp.float32).astype(
        jnp.bfloat16
    )
    back_mixed = lax.dot_general(
        landed_cotangent,
        output_weight,
        (((1,), (1,)), ((), ())),
        preferred_element_type=jnp.float32,
    ).astype(jnp.bfloat16)
    back_packed = central_gather(back_mixed)[0]
    back_normed = lax.dot_general(
        back_packed, input_weight, (((1,), (1,)), ((), ())), preferred_element_type=jnp.float32
    )
    back_rows = norm_pull(back_normed)[0]
    return (result, back_rows, normed_half, back_packed, merged_rows)


def contract(left_part, right_part):
    return lax.dot_general(
        left_part, right_part, (((0,), (0,)), ((), ())), preferred_element_type=jnp.float32
    )


def ordered_contract(left_part, right_part, replicas, owners):
    rows, features = left_part.shape
    per_device = features // owners // replicas
    flipped = jnp.transpose(left_part).reshape(owners, replicas, per_device * rows)
    flipped = jnp.swapaxes(flipped, 0, 1).reshape(features, rows)
    return jnp.dot(flipped, right_part, preferred_element_type=jnp.float32)


def dense_all_to_all(pieces, axis_name):
    count = pieces.shape[0]
    flat = pieces.reshape(count, -1, 128)
    moved = lax.all_to_all(flat, axis_name, 0, 0, tiled=True)
    return moved.reshape(pieces.shape)


def reduce_weight_terms(partial, replicas, owners):
    rows, width = partial.shape
    per_replica = rows // replicas
    per_device = per_replica // owners
    terms = partial.astype(jnp.bfloat16).reshape(replicas, per_replica, width)
    terms = lax.all_to_all(terms, "dp", 0, 0, tiled=True)
    terms = jnp.sum(terms.astype(jnp.float32), axis=0).astype(jnp.bfloat16)
    terms = terms.reshape(owners, per_device, width)
    terms = dense_all_to_all(terms, "ev")
    piece = jnp.sum(terms.astype(jnp.float32), axis=0)
    copies = jnp.broadcast_to(piece[None], (replicas, per_device, width))
    gathered = dense_all_to_all(copies, "dp")
    return gathered.reshape(replicas * per_device, width)


def on_device(
    events,
    cotangent,
    intra_gain,
    intra_proj,
    intra_out,
    cross_norm_gain,
    cross_input_weight,
    cross_output_weight,
    owner_map,
    block_lists,
):
    rows_here = events[0]
    upstream = cotangent[0]
    local_rows, features = rows_here.shape
    owners = lax.axis_size("ev")
    replicas = lax.axis_size("dp")
    own_index = lax.axis_index("ev")
    row_capacity = 2 * local_rows // owners
    buffer_rows = owners * row_capacity
    hidden, intra_pull = jax.vjp(
        lambda input_operand: intra_branch(input_operand, intra_gain, intra_proj, intra_out),
        rows_here,
    )
    targets = owner_map[0]
    onehot = (targets[:, None] == jnp.arange(owners, dtype=jnp.int32)[None, :]).astype(jnp.int32)
    row_counts = jnp.sum(onehot.reshape(owners, local_rows, owners), axis=1)
    inbound_rows = lax.dynamic_index_in_dim(row_counts, own_index, axis=1, keepdims=False)
    own_onehot = lax.dynamic_slice_in_dim(onehot, own_index * local_rows, local_rows, 0)
    before = jnp.cumsum(own_onehot, axis=0) - own_onehot
    slot_ids = jnp.sum(before * own_onehot, axis=1)
    own_dest = lax.dynamic_slice_in_dim(targets, own_index * local_rows, local_rows, 0)
    position = own_dest * row_capacity + slot_ids
    placement = (
        jnp.arange(buffer_rows, dtype=jnp.int32)[:, None] == position[None, :]
    ).astype(jnp.bfloat16)
    both = jnp.concatenate([hidden, upstream], axis=1)
    outgoing = jnp.dot(placement, both, preferred_element_type=jnp.float32).astype(jnp.bfloat16)
    landed = lax.all_to_all(outgoing, "ev", split_axis=0, concat_axis=0, tiled=True)
    landed_rows = landed[:, :features]
    landed_cotangent = landed[:, features:]
    row_presence = (
        jnp.arange(row_capacity, dtype=jnp.int32)[None, :] < inbound_rows[:, None]
    ).reshape(buffer_rows)
    block_listing = block_lists[0, 0]
    result, back_rows, normed_half, back_packed, merged_rows = owner_transfer(
        landed_rows,
        landed_cotangent,
        row_presence,
        block_listing,
        cross_norm_gain,
        cross_input_weight,
        cross_output_weight,
    )
    going_back = jnp.concatenate([result, back_rows.astype(jnp.bfloat16)], axis=1)
    came_back = lax.all_to_all(going_back, "ev", split_axis=0, concat_axis=0, tiled=True)
    picked = lax.dot_general(
        placement, came_back, (((0,), (0,)), ((), ())), preferred_element_type=jnp.float32
    )
    layer_out = (hidden.astype(jnp.float32) + picked[:, :features]).astype(jnp.bfloat16)
    grad_hidden = (upstream.astype(jnp.float32) + picked[:, features:]).astype(jnp.bfloat16)
    grad_rows = intra_pull(grad_hidden)[0]
    factor = (replicas * owners * local_rows) ** (-0.5)
    partial_sum = jnp.concatenate(
        [
            ordered_contract(normed_half, back_packed, replicas, owners),
            ordered_contract(merged_rows, landed_cotangent, replicas, owners),
        ],
        axis=1,
    )
    portion = reduce_weight_terms(partial_sum, replicas, owners) * factor
    return (
        layer_out[None],
        grad_rows[None],
        portion[:, : 3 * features],
        portion[:, 3 * features :],
    )


def solution(mesh):
    return jax.shard_map(
        on_device,
        mesh=mesh,
        in_specs=(
            P("dp", "ev", None),
            P("dp", "ev", None),
            P(),
            P(),
            P(),
            P(),
            P(),
            P(),
            P("dp", None),
            P("dp", "ev", None, None),
        ),
        out_specs=(P("dp", "ev", None), P("dp", "ev", None), P("ev", None), P("ev", None)),
        check_vma=False,
    )
```
